32 devices in a mesh: dp: 8 (over z, y), tensor: 4 (over x, core).
Axes of the slice: x: 2, y: 2, z: 4, core: 2. Of those that a mesh axis runs over, the one named last changes fastest.
Arguments:
- tokens: bfloat16 [8, 1024, 1536], P('dp'), may hold values from -6 to 6
- piece_starts: int32 [8, 2], P('dp'), may hold values from -1 to 768, as said below
- attn_gain: bfloat16 [1536], P('dp'), may hold values from 0.5 to 1.5
- w_query: bfloat16 [1536, 1536], P('dp', 'tensor'), may hold values from -0.15625 to 0.15625
- w_key: bfloat16 [1536, 1536], P('dp', 'tensor'), may hold values from -0.15625 to 0.15625
- w_value: bfloat16 [1536, 1536], P('dp', 'tensor'), may hold values from -0.15625 to 0.15625
- w_outgate: bfloat16 [1536, 1536], P('dp', 'tensor'), may hold values from -0.15625 to 0.15625
- w_forget: bfloat16 [1536, 24], P('dp', 'tensor'), may hold values from -0.3125 to 0.3125
- forget_bias: float32 [24], P('tensor'), may hold values from 2 to 8
- w_output: bfloat16 [1536, 1536], P('tensor', 'dp'), may hold values from -0.4375 to 0.4375
- ffn_gain: bfloat16 [1536], P('dp'), may hold values from 0.5 to 1.5
- w_gate: bfloat16 [1536, 4096], P('dp', 'tensor'), may hold values from -0.15625 to 0.15625
- w_up: bfloat16 [1536, 4096], P('dp', 'tensor'), may hold values from -0.15625 to 0.15625
- w_down: bfloat16 [4096, 1536], P('tensor', 'dp'), may hold values from -0.09375 to 0.09375
- cotangent: bfloat16 [8, 1024, 1536], P('dp'), may hold values from -6 to 6
Outputs:
- output: bfloat16 [8, 1024, 1536], P('dp')
- tokens_grad: bfloat16 [8, 1024, 1536], P('dp')
- attn_gain_grad: float32 [1536], P('dp')
- w_query_grad: float32 [1536, 1536], P('dp', 'tensor')
- w_key_grad: float32 [1536, 1536], P('dp', 'tensor')
- w_value_grad: float32 [1536, 1536], P('dp', 'tensor')
- w_outgate_grad: float32 [1536, 1536], P('dp', 'tensor')
- w_forget_grad: float32 [1536, 24], P('dp', 'tensor')
- forget_bias_grad: float32 [24], P('tensor')
- w_output_grad: float32 [1536, 1536], P('tensor', 'dp')
- ffn_gain_grad: float32 [1536], P('dp')
- w_gate_grad: float32 [1536, 4096], P('dp', 'tensor')
- w_up_grad: float32 [1536, 4096], P('dp', 'tensor')
- w_down_grad: float32 [4096, 1536], P('tensor', 'dp')
The draws below stay inside these ranges and needn't reach their ends.
Inputs may be any that keep to these rules, and one draw needn't show every extreme that they name: `piece_starts`: slot k of a sequence's row holds -1 (no piece) or a start in [k * 512, (k + 1) * 512 - 256], so pieces never intersect; the number of pieces differs between sequences.
All inputs are finite; a program needn't handle non-finite values.
Results may differ from the reference program's by a relative error of at most 0.025.
Values may be sent and summed in bfloat16 or wider, within the bound.
No kernel may reach another device: no remote copies, remote signals or barrier semaphores. Data moves between devices by JAX's collectives and lax.ppermute only.
A program may use at most 256 MiB of HBM per device.

```python
import jax
import jax.numpy as jnp
from jax import lax

D = 1536
HEADS = 24
HEAD_DIM = 64
FF = 4096
SEQ_LEN = 1024
PIECE = 256
SLOTS = 2
SEQUENCES = 8
N_TENSOR = 4


def draw_piece_starts(key, part):
    slot_width = SEQ_LEN // SLOTS
    key_use, key_where = jax.random.split(jax.random.fold_in(key, 11))
    present = jax.random.randint(key_use, (SEQUENCES, SLOTS), 0, 2)
    offsets = jax.random.randint(key_where, (SEQUENCES, SLOTS), 0, slot_width - PIECE + 1)
    slot_index = jnp.arange(SLOTS, dtype=jnp.int32)[None, :]
    row_index = jnp.arange(SEQUENCES, dtype=jnp.int32)[:, None]
    present = jnp.where(row_index == 0, (slot_index == SLOTS - 1).astype(jnp.int32), present)
    present = jnp.where(row_index == 1, 1, present)
    offsets = jnp.where(row_index == 0, slot_width - PIECE, offsets)
    return jnp.where(present > 0, slot_index * slot_width + offsets, -1).astype(jnp.int32)


def levels(stream_key, extent, pieces, smallest, top_value):
    def one(axis_at, blocks):
        steps = jax.random.uniform(jax.random.fold_in(jax.random.fold_in(stream_key, 6), axis_at), (blocks,), jnp.float32, smallest / len(pieces), top_value / len(pieces))
        return jnp.repeat(jnp.exp(steps), extent[axis_at] // blocks).reshape((-1,) + (1,) * (len(extent) - axis_at - 1))

    loudness = one(*pieces[0])
    for cut in pieces[1:]:
        loudness = loudness * one(*cut)
    return loudness


def centred(rng, shape, scale, bound, shards=(), kind=jnp.bfloat16):
    loudness = levels(rng, shape, shards, -0.22, 0.18) if shards else 1.0
    entries = jax.random.normal(rng, shape, jnp.float32) * scale * loudness
    return jnp.minimum(jnp.maximum(entries, -bound), bound).astype(kind)


def setup_inputs(seed: int = 0) -> dict:
    keys = jax.random.split(jax.random.key(seed), 16)
    return {
        "tokens": centred(keys[0], (SEQUENCES, SEQ_LEN, D), 1.0, 6.0, ((0, 8),)),
        "piece_starts": draw_piece_starts(jax.random.fold_in(keys[15], 71), 0),
        "attn_gain": jnp.clip(1.0 + 0.1 * jax.random.normal(keys[2], (D,), jnp.float32), 0.5, 1.5).astype(jnp.bfloat16),
        "w_query": centred(keys[3], (D, D), D ** -0.5, 0.15625, ((0, 8), (1, 4))),
        "w_key": centred(keys[4], (D, D), D ** -0.5, 0.15625, ((0, 8), (1, 4))),
        "w_value": centred(keys[5], (D, D), D ** -0.5, 0.15625, ((0, 8), (1, 4))),
        "w_outgate": centred(keys[6], (D, D), D ** -0.5, 0.15625, ((0, 8), (1, 4))),
        "w_forget": centred(keys[7], (D, HEADS), (D // 4) ** -0.5, 0.3125, ((0, 8), (1, 4))),
        "forget_bias": jnp.clip(2.0 + 6.0 * jax.random.uniform(keys[8], (HEADS,), jnp.float32) ** levels(keys[8], (HEADS,), ((0, 4),), -0.2, 0.2), 2.0, 8.0),
        "w_output": centred(keys[9], (D, D), (D // 8) ** -0.5, 0.4375, ((0, 4), (1, 8))),
        "ffn_gain": jnp.clip(1.0 + 0.1 * jax.random.normal(keys[10], (D,), jnp.float32), 0.5, 1.5).astype(jnp.bfloat16),
        "w_gate": centred(keys[11], (D, FF), D ** -0.5, 0.15625, ((0, 8), (1, 4))),
        "w_up": centred(keys[12], (D, FF), D ** -0.5, 0.15625, ((0, 8), (1, 4))),
        "w_down": centred(keys[13], (FF, D), FF ** -0.5, 0.09375, ((0, 4), (1, 8))),
        "cotangent": centred(keys[14], (SEQUENCES, SEQ_LEN, D), 1.0, 6.0, ((0, 8),)),
    }


epsilon = 1e-06
masked_value = -1e+30

@jax.custom_vjp
def low(v):
    return lax.optimization_barrier(v.astype(jnp.bfloat16)).astype(jnp.float32)

@jax.custom_vjp
def low_back(v):
    return v

def low_keep(v):
    return (low(v), None)

def low_pass(kept, grad):
    return (grad,)

def back_keep(v):
    return (v, None)

def back_low(kept, grad):
    return (low(grad),)
low.defvjp(low_keep, low_pass)
low_back.defvjp(back_keep, back_low)

def matmul(left, right):
    return jnp.dot(left, right, precision=lax.Precision.HIGHEST, preferred_element_type=jnp.float32)

def normalize(values, gain):
    return values * lax.rsqrt(lax.optimization_barrier(jnp.mean(values * values, axis=-1, keepdims=True)) + epsilon) * gain

def allowed_pairs(starts):
    places = jnp.arange(SEQ_LEN, dtype=jnp.int32)
    inside = (starts[:, None] >= 0) & (places[None, :] >= starts[:, None]) & (places[None, :] < starts[:, None] + PIECE)
    labels = lax.optimization_barrier(jnp.sum(jnp.where(inside, jnp.arange(1, SLOTS + 1, dtype=jnp.int32)[:, None], 0), axis=0))
    same = (labels[:, None] == labels[None, :]) & (labels[:, None] > 0)
    return (places[None, :] <= places[:, None]) | same

def attend(query_rows, key_rows, value_rows, log_forget, allowed):
    raw = jnp.einsum('qhd,khd->hqk', query_rows, key_rows, precision=lax.Precision.HIGHEST) * HEAD_DIM ** (-0.5)
    raw = low_back(raw)
    decay = jnp.cumsum(log_forget, axis=0).T
    scores = raw - jnp.abs(decay[:, :, None] - decay[:, None, :])
    scores = jnp.where(allowed[None], scores, masked_value)
    chances = jax.nn.softmax(scores, axis=-1)
    return jnp.einsum('hqk,khd->qhd', low(chances), value_rows, precision=lax.Precision.HIGHEST)

def layer(inputs, starts, attn_gain, w_query, w_key, w_value, w_outgate, w_forget, forget_bias, w_output, ffn_gain, w_gate, w_up, w_down):
    allowed = allowed_pairs(starts)
    width = D // N_TENSOR
    heads_here = HEADS // N_TENSOR
    units = FF // N_TENSOR
    normed = low(normalize(inputs, attn_gain))
    attention = jnp.zeros_like(inputs)
    for group in range(N_TENSOR):
        columns = slice(group * width, (group + 1) * width)
        head_cols = slice(group * heads_here, (group + 1) * heads_here)
        shared = low_back(normed)
        query_rows = low(low_back(matmul(shared, w_query[:, columns]))).reshape(SEQ_LEN, heads_here, HEAD_DIM)
        key_rows = low(low_back(matmul(shared, w_key[:, columns]))).reshape(SEQ_LEN, heads_here, HEAD_DIM)
        value_rows = low(low_back(matmul(shared, w_value[:, columns]))).reshape(SEQ_LEN, heads_here, HEAD_DIM)
        gate_pre = low_back(matmul(shared, w_outgate[:, columns]))
        forget_pre = low_back(matmul(shared, w_forget[:, head_cols]) + forget_bias[head_cols])
        attended = low_back(attend(query_rows, key_rows, value_rows, jax.nn.log_sigmoid(forget_pre), allowed))
        gated = low(attended.reshape(SEQ_LEN, width) * jax.nn.sigmoid(gate_pre))
        attention = attention + low(matmul(gated, w_output[columns, :]))
    hidden = inputs + low_back(attention)
    normed2 = low(normalize(hidden, ffn_gain))
    ffn = jnp.zeros_like(inputs)
    for group in range(N_TENSOR):
        columns = slice(group * units, (group + 1) * units)
        shared = low_back(normed2)
        gate_part = low_back(matmul(shared, w_gate[:, columns]))
        up_part = low_back(matmul(shared, w_up[:, columns]))
        inner = low(jax.nn.silu(gate_part) * up_part)
        ffn = ffn + low(matmul(inner, w_down[columns, :]))
    return hidden + low_back(ffn)

def reference(tokens, piece_starts, attn_gain, w_query, w_key, w_value, w_outgate, w_forget, forget_bias, w_output, ffn_gain, w_gate, w_up, w_down, cotangent):
    weights = tuple((w.astype(jnp.float32) for w in (attn_gain, w_query, w_key, w_value, w_outgate, w_forget, forget_bias, w_output, ffn_gain, w_gate, w_up, w_down)))

    def one_sequence(sums, items):
        inputs, starts, upstream = items

        def forward(inputs_f, *params):
            return layer(inputs_f, starts, *params)
        result, pullback = jax.vjp(forward, inputs.astype(jnp.float32), *weights)
        grads = pullback(upstream.astype(jnp.float32))
        sums = tuple((earlier + update for earlier, update in zip(sums, grads[1:])))
        return (sums, (result.astype(jnp.bfloat16), grads[0].astype(jnp.bfloat16)))
    initial = tuple((jnp.zeros_like(w) for w in weights))
    sums, outputs = lax.scan(one_sequence, initial, (tokens, piece_starts, cotangent))
    return (outputs[0], outputs[1], sums[0], sums[1], sums[2], sums[3], sums[4], sums[5], sums[6], sums[7], sums[8], sums[9], sums[10], sums[11])
```

```python
import jax
import jax.numpy as jnp
from jax import lax
from jax.sharding import PartitionSpec as P

PIECE = 256


epsilon = 1e-06
masked_value = -1e30


def project(left, right):
    return jnp.dot(left, right, preferred_element_type=jnp.float32)


def contract_rows(left, right):
    return lax.dot_general(
        left, right, (((0,), (0,)), ((), ())), preferred_element_type=jnp.float32
    )


def contract_cols(left, right):
    return lax.dot_general(
        left, right, (((1,), (1,)), ((), ())), preferred_element_type=jnp.float32
    )


def allowed_pairs(starts, length):
    places = jnp.arange(length, dtype=jnp.int32)
    inside = (
        (starts[:, None] >= 0)
        & (places[None, :] >= starts[:, None])
        & (places[None, :] < starts[:, None] + PIECE)
    )
    labels = jnp.sum(
        jnp.where(inside, jnp.arange(1, starts.shape[0] + 1, dtype=jnp.int32)[:, None], 0), axis=0
    )
    same = (labels[:, None] == labels[None, :]) & (labels[:, None] > 0)
    return (places[None, :] <= places[:, None]) | same


def block_scores(query_rows, key_all, decay, allowed_rows, first_row):
    count = query_rows.shape[0]
    raw = jnp.einsum(
        "qhd,khd->hqk", query_rows, key_all, preferred_element_type=jnp.float32
    ) * query_rows.shape[-1] ** (-0.5)
    apart = (
        lax.slice_in_dim(decay, first_row, first_row + count, axis=1)[:, :, None]
        - decay[:, None, :]
    )
    return (jnp.where(allowed_rows[None], raw - jnp.abs(apart), masked_value), apart)


def attend_forward(items):
    query_all, key_all, value_all, log_forget, starts = items
    length = query_all.shape[0]
    block_rows = min(512, length)
    decay = jnp.cumsum(log_forget, axis=0).T
    allowed = allowed_pairs(starts, length)
    results = []
    normalizers = []
    for first_row in range(0, length, block_rows):
        scores, apart = block_scores(
            query_all[first_row : first_row + block_rows],
            key_all,
            decay,
            allowed[first_row : first_row + block_rows],
            first_row,
        )
        largest = jnp.max(scores, axis=-1, keepdims=True)
        weights = jnp.exp(scores - largest)
        denominator = jnp.sum(weights, axis=-1, keepdims=True)
        chances = (weights / denominator).astype(jnp.bfloat16)
        results.append(
            jnp.einsum("hqk,khd->qhd", chances, value_all, preferred_element_type=jnp.float32)
        )
        normalizers.append(largest + jnp.log(denominator))
    return (jnp.concatenate(results, axis=0), jnp.concatenate(normalizers, axis=1))


def attend_backward(items):
    query_all, key_all, value_all, log_forget, starts, attended, normalizer, grad_out = items
    length = query_all.shape[0]
    block_rows = min(512, length)
    scale = query_all.shape[-1] ** (-0.5)
    decay = jnp.cumsum(log_forget, axis=0).T
    allowed = allowed_pairs(starts, length)
    grad_key = jnp.zeros(key_all.shape, jnp.float32)
    grad_value = jnp.zeros(value_all.shape, jnp.float32)
    grad_decay = jnp.zeros(decay.shape, jnp.float32)
    query_parts = []
    row_parts = []
    for first_row in range(0, length, block_rows):
        query_rows = query_all[first_row : first_row + block_rows]
        out_rows = grad_out[first_row : first_row + block_rows]
        scores, apart = block_scores(
            query_rows, key_all, decay, allowed[first_row : first_row + block_rows], first_row
        )
        chances = jnp.exp(scores - normalizer[:, first_row : first_row + block_rows])
        grad_chance = jnp.einsum(
            "qhd,khd->hqk", out_rows, value_all, preferred_element_type=jnp.float32
        )
        offset = jnp.sum(
            out_rows.astype(jnp.float32) * attended[first_row : first_row + block_rows], axis=-1
        ).T[:, :, None]
        grad_score = chances * (grad_chance - offset)
        grad_rounded = grad_score.astype(jnp.bfloat16)
        grad_value = grad_value + jnp.einsum(
            "hqk,qhd->khd",
            chances.astype(jnp.bfloat16),
            out_rows,
            preferred_element_type=jnp.float32,
        )
        grad_key = (
            grad_key
            + jnp.einsum(
                "hqk,qhd->khd", grad_rounded, query_rows, preferred_element_type=jnp.float32
            )
            * scale
        )
        query_parts.append(
            jnp.einsum("hqk,khd->qhd", grad_rounded, key_all, preferred_element_type=jnp.float32)
            * scale
        )
        signed = grad_score * jnp.sign(apart)
        grad_decay = grad_decay + jnp.sum(signed, axis=1)
        row_parts.append(-jnp.sum(signed, axis=-1))
    grad_decay = grad_decay + jnp.concatenate(row_parts, axis=1)
    grad_log = jnp.flip(jnp.cumsum(jnp.flip(grad_decay, axis=1), axis=1), axis=1).T
    grad_query = jnp.concatenate(query_parts, axis=0)
    return (
        grad_query.astype(jnp.bfloat16),
        grad_key.astype(jnp.bfloat16),
        grad_value.astype(jnp.bfloat16),
        grad_log,
    )


def on_device(
    tokens,
    piece_starts,
    attn_gain,
    w_query,
    w_key,
    w_value,
    w_outgate,
    w_forget,
    forget_bias,
    w_output,
    ffn_gain,
    w_gate,
    w_up,
    w_down,
    cotangent,
):
    sequences, length, width = tokens.shape
    heads_here = w_forget.shape[1]
    share_width = w_query.shape[1]
    head_size = share_width // heads_here
    row_count = sequences * length
    block = w_query.shape[0]
    units = w_gate.shape[1]

    def head_view(values):
        return values.reshape(sequences, length, heads_here, head_size)

    attn_local = jnp.concatenate(
        [w_query, w_key, w_value, w_outgate, w_output.T, w_forget, attn_gain[:, None]], axis=1
    )
    attn_full = lax.all_gather(attn_local, "dp", axis=0, tiled=True)
    joined = attn_full[:, : 4 * share_width]
    output_t = attn_full[:, 4 * share_width : 5 * share_width]
    forget_w = attn_full[:, 5 * share_width : 5 * share_width + heads_here]
    gain_one = attn_full[:, 5 * share_width + heads_here].astype(jnp.float32)
    ffn_local = jnp.concatenate([w_gate, w_up, w_down.T, ffn_gain[:, None]], axis=1)
    ffn_full = lax.all_gather(ffn_local, "dp", axis=0, tiled=True)
    gate_up_w = ffn_full[:, : 2 * units]
    down_t = ffn_full[:, 2 * units : 3 * units]
    gain_two = ffn_full[:, 3 * units].astype(jnp.float32)

    inputs = tokens.reshape(row_count, width).astype(jnp.float32)
    scale_one = lax.rsqrt(jnp.mean(inputs * inputs, axis=-1, keepdims=True) + epsilon)
    unit_one = inputs * scale_one
    normed = (unit_one * gain_one).astype(jnp.bfloat16)
    projected = project(normed, joined)
    query_all = head_view(projected[:, :share_width].astype(jnp.bfloat16))
    key_all = head_view(projected[:, share_width : 2 * share_width].astype(jnp.bfloat16))
    value_all = head_view(projected[:, 2 * share_width : 3 * share_width].astype(jnp.bfloat16))
    gate_pre = projected[:, 3 * share_width :]
    forget_pre = project(normed, forget_w) + forget_bias[None, :]
    log_forget = jax.nn.log_sigmoid(forget_pre).reshape(sequences, length, heads_here)
    attended, normalizer = lax.map(
        attend_forward, (query_all, key_all, value_all, log_forget, piece_starts)
    )
    attended_flat = attended.reshape(row_count, share_width)
    gate_open = jax.nn.sigmoid(gate_pre)
    gated = (attended_flat * gate_open).astype(jnp.bfloat16)
    attention = lax.psum(contract_cols(gated, output_t).astype(jnp.bfloat16), "tensor").astype(
        jnp.float32
    )
    hidden = inputs + attention
    scale_two = lax.rsqrt(jnp.mean(hidden * hidden, axis=-1, keepdims=True) + epsilon)
    unit_two = hidden * scale_two
    normed_two = (unit_two * gain_two).astype(jnp.bfloat16)
    inner_pre = project(normed_two, gate_up_w)
    gate_part = inner_pre[:, :units]
    up_part = inner_pre[:, units:]
    inner = (jax.nn.silu(gate_part) * up_part).astype(jnp.bfloat16)
    ffn_out = lax.psum(contract_cols(inner, down_t).astype(jnp.bfloat16), "tensor").astype(
        jnp.float32
    )
    output = (hidden + ffn_out).astype(jnp.bfloat16).reshape(tokens.shape)
    upstream_low = cotangent.reshape(row_count, width)
    upstream = upstream_low.astype(jnp.float32)
    grad_down_t = contract_rows(upstream_low, inner)
    grad_inner = project(upstream_low, down_t)
    sigma = jax.nn.sigmoid(gate_part)
    grad_gate = (grad_inner * up_part * sigma * (1.0 + gate_part * (1.0 - sigma))).astype(
        jnp.bfloat16
    )
    grad_up = (grad_inner * gate_part * sigma).astype(jnp.bfloat16)
    grad_gate_up = jnp.concatenate([grad_gate, grad_up], axis=1)
    grad_gate_up_w = contract_rows(normed_two, grad_gate_up)
    grad_normed_two = lax.psum(
        contract_cols(grad_gate_up, gate_up_w).astype(jnp.bfloat16), "tensor"
    ).astype(jnp.float32)
    grad_ffn_gain = jnp.sum(grad_normed_two * unit_two, axis=0)
    ffn_sums = lax.psum_scatter(
        jnp.concatenate(
            [grad_gate_up_w, grad_down_t, grad_ffn_gain[:, None]], axis=1
        ).astype(jnp.bfloat16),
        "dp",
        scatter_dimension=0,
        tiled=True,
    ).astype(jnp.float32)
    grad_unit_two = grad_normed_two * gain_two
    grad_hidden = upstream + scale_two * (
        grad_unit_two - unit_two * jnp.mean(grad_unit_two * unit_two, axis=-1, keepdims=True)
    )
    hidden_low = grad_hidden.astype(jnp.bfloat16)
    grad_output_t = contract_rows(hidden_low, gated)
    grad_gated = project(hidden_low, output_t)
    grad_attended = (grad_gated * gate_open).astype(jnp.bfloat16)
    grad_gate_pre = (grad_gated * attended_flat * gate_open * (1.0 - gate_open)).astype(
        jnp.bfloat16
    )
    grad_query, grad_key, grad_value, grad_log = lax.map(
        attend_backward,
        (
            query_all,
            key_all,
            value_all,
            log_forget,
            piece_starts,
            attended,
            normalizer,
            head_view(grad_attended),
        ),
    )
    grad_forget = (grad_log.reshape(row_count, heads_here) * jax.nn.sigmoid(-forget_pre)).astype(
        jnp.bfloat16
    )
    grad_four = jnp.concatenate(
        [
            grad_query.reshape(row_count, share_width),
            grad_key.reshape(row_count, share_width),
            grad_value.reshape(row_count, share_width),
            grad_gate_pre,
        ],
        axis=1,
    )
    grad_joined = contract_rows(normed, grad_four)
    grad_forget_w = contract_rows(normed, grad_forget)
    grad_bias = jnp.sum(grad_forget.astype(jnp.float32), axis=0)
    grad_normed = lax.psum(
        (contract_cols(grad_four, joined) + contract_cols(grad_forget, forget_w)).astype(
            jnp.bfloat16
        ),
        "tensor",
    ).astype(jnp.float32)
    grad_attn_gain = jnp.sum(grad_normed * unit_one, axis=0)
    grad_unit_one = grad_normed * gain_one
    grad_inputs = grad_hidden + scale_one * (
        grad_unit_one - unit_one * jnp.mean(grad_unit_one * unit_one, axis=-1, keepdims=True)
    )
    tokens_grad = grad_inputs.astype(jnp.bfloat16).reshape(tokens.shape)
    place = jnp.arange(width, dtype=jnp.int32) % block
    bias_col = jnp.where(
        place < heads_here, jnp.take(grad_bias, jnp.minimum(place, heads_here - 1)), 0.0
    )
    attn_sums = lax.psum_scatter(
        jnp.concatenate(
            [grad_joined, grad_output_t, grad_forget_w, grad_attn_gain[:, None], bias_col[:, None]],
            axis=1,
        ).astype(jnp.bfloat16),
        "dp",
        scatter_dimension=0,
        tiled=True,
    ).astype(jnp.float32)
    forget_at = 5 * share_width
    return (
        output,
        tokens_grad,
        attn_sums[:, forget_at + heads_here],
        attn_sums[:, :share_width],
        attn_sums[:, share_width : 2 * share_width],
        attn_sums[:, 2 * share_width : 3 * share_width],
        attn_sums[:, 3 * share_width : 4 * share_width],
        attn_sums[:, forget_at : forget_at + heads_here],
        attn_sums[:heads_here, forget_at + heads_here + 1],
        attn_sums[:, 4 * share_width : 5 * share_width].T,
        ffn_sums[:, 3 * units],
        ffn_sums[:, :units],
        ffn_sums[:, units : 2 * units],
        ffn_sums[:, 2 * units : 3 * units].T,
    )


def solution(mesh):
    placed = (
        P("dp", None, None),
        P("dp", None),
        P("dp"),
        P("dp", "tensor"),
        P("dp", "tensor"),
        P("dp", "tensor"),
        P("dp", "tensor"),
        P("dp", "tensor"),
        P("tensor"),
        P("tensor", "dp"),
        P("dp"),
        P("dp", "tensor"),
        P("dp", "tensor"),
        P("tensor", "dp"),
        P("dp", None, None),
    )
    return jax.shard_map(
        on_device,
        mesh=mesh,
        in_specs=placed,
        out_specs=(
            P("dp", None, None),
            P("dp", None, None),
            P("dp"),
            P("dp", "tensor"),
            P("dp", "tensor"),
            P("dp", "tensor"),
            P("dp", "tensor"),
            P("dp", "tensor"),
            P("tensor"),
            P("tensor", "dp"),
            P("dp"),
            P("dp", "tensor"),
            P("dp", "tensor"),
            P("tensor", "dp"),
        ),
        check_vma=False,
    )
```

```python
import jax
import jax.numpy as jnp
from jax import lax
from jax.sharding import PartitionSpec as P

PIECE = 256


epsilon = 1e-06
masked_value = -1e30


def project(left, right):
    return jnp.dot(left, right, preferred_element_type=jnp.float32)


def contract_rows(left, right):
    return lax.dot_general(
        left, right, (((0,), (0,)), ((), ())), preferred_element_type=jnp.float32
    )


def contract_cols(left, right):
    return lax.dot_general(
        left, right, (((1,), (1,)), ((), ())), preferred_element_type=jnp.float32
    )


def allowed_pairs(starts, length):
    places = jnp.arange(length, dtype=jnp.int32)
    inside = (
        (starts[:, None] >= 0)
        & (places[None, :] >= starts[:, None])
        & (places[None, :] < starts[:, None] + PIECE)
    )
    labels = jnp.sum(
        jnp.where(inside, jnp.arange(1, starts.shape[0] + 1, dtype=jnp.int32)[:, None], 0), axis=0
    )
    same = (labels[:, None] == labels[None, :]) & (labels[:, None] > 0)
    return (places[None, :] <= places[:, None]) | same


def block_scores(query_rows, key_all, decay, allowed_rows, first_row):
    count = query_rows.shape[0]
    raw = jnp.einsum(
        "qhd,khd->hqk", query_rows, key_all, preferred_element_type=jnp.float32
    ) * query_rows.shape[-1] ** (-0.5)
    apart = (
        lax.slice_in_dim(decay, first_row, first_row + count, axis=1)[:, :, None]
        - decay[:, None, :]
    )
    return (jnp.where(allowed_rows[None], raw - jnp.abs(apart), masked_value), apart)


def attend_forward(items):
    query_all, key_all, value_all, log_forget, starts = items
    length = query_all.shape[0]
    block_rows = min(512, length)
    decay = jnp.cumsum(log_forget, axis=0).T
    allowed = allowed_pairs(starts, length)
    results = []
    normalizers = []
    for first_row in range(0, length, block_rows):
        scores, apart = block_scores(
            query_all[first_row : first_row + block_rows],
            key_all,
            decay,
            allowed[first_row : first_row + block_rows],
            first_row,
        )
        largest = jnp.max(scores, axis=-1, keepdims=True)
        weights = jnp.exp(scores - largest)
        denominator = jnp.sum(weights, axis=-1, keepdims=True)
        chances = (weights / denominator).astype(jnp.bfloat16)
        results.append(
            jnp.einsum("hqk,khd->qhd", chances, value_all, preferred_element_type=jnp.float32)
        )
        normalizers.append(largest + jnp.log(denominator))
    return (jnp.concatenate(results, axis=0), jnp.concatenate(normalizers, axis=1))


def attend_backward(items):
    query_all, key_all, value_all, log_forget, starts, attended, normalizer, grad_out = items
    length = query_all.shape[0]
    block_rows = min(512, length)
    scale = query_all.shape[-1] ** (-0.5)
    decay = jnp.cumsum(log_forget, axis=0).T
    allowed = allowed_pairs(starts, length)
    grad_key = jnp.zeros(key_all.shape, jnp.float32)
    grad_value = jnp.zeros(value_all.shape, jnp.float32)
    grad_decay = jnp.zeros(decay.shape, jnp.float32)
    query_parts = []
    row_parts = []
    for first_row in range(0, length, block_rows):
        query_rows = query_all[first_row : first_row + block_rows]
        out_rows = grad_out[first_row : first_row + block_rows]
        scores, apart = block_scores(
            query_rows, key_all, decay, allowed[first_row : first_row + block_rows], first_row
        )
        chances = jnp.exp(scores - normalizer[:, first_row : first_row + block_rows])
        grad_chance = jnp.einsum(
            "qhd,khd->hqk", out_rows, value_all, preferred_element_type=jnp.float32
        )
        offset = jnp.sum(
            out_rows.astype(jnp.float32) * attended[first_row : first_row + block_rows], axis=-1
        ).T[:, :, None]
        grad_score = chances * (grad_chance - offset)
        grad_rounded = grad_score.astype(jnp.bfloat16)
        grad_value = grad_value + jnp.einsum(
            "hqk,qhd->khd",
            chances.astype(jnp.bfloat16),
            out_rows,
            preferred_element_type=jnp.float32,
        )
        grad_key = (
            grad_key
            + jnp.einsum(
                "hqk,qhd->khd", grad_rounded, query_rows, preferred_element_type=jnp.float32
            )
            * scale
        )
        query_parts.append(
            jnp.einsum("hqk,khd->qhd", grad_rounded, key_all, preferred_element_type=jnp.float32)
            * scale
        )
        signed = grad_score * jnp.sign(apart)
        grad_decay = grad_decay + jnp.sum(signed, axis=1)
        row_parts.append(-jnp.sum(signed, axis=-1))
    grad_decay = grad_decay + jnp.concatenate(row_parts, axis=1)
    grad_log = jnp.flip(jnp.cumsum(jnp.flip(grad_decay, axis=1), axis=1), axis=1).T
    grad_query = jnp.concatenate(query_parts, axis=0)
    return (
        grad_query.astype(jnp.bfloat16),
        grad_key.astype(jnp.bfloat16),
        grad_value.astype(jnp.bfloat16),
        grad_log,
    )


def ring_order(n):
    inner = 2 if n % 2 == 0 else 1
    outer = n // inner
    order = [o * inner for o in range(outer)]
    if inner == 2:
        order += [o * inner + 1 for o in reversed(range(outer))]
    return order


def ring_tables(n):
    order = ring_order(n)
    where = [0] * n
    for p, d in enumerate(order):
        where[d] = p
    to_next = [(order[p], order[(p + 1) % n]) for p in range(n)]
    to_prev = [(order[p], order[(p - 1) % n]) for p in range(n)]
    return order, where, to_next, to_prev


def ring_gather(local, axis):
    n = lax.axis_size(axis)
    rows = local.shape[0]
    if n > 16:
        return lax.all_gather(local, axis, axis=0, tiled=True)
    order, where, to_next, to_prev = ring_tables(n)
    me = lax.axis_index(axis)
    out = jnp.zeros((n, rows) + local.shape[1:], local.dtype)
    out = lax.dynamic_update_index_in_dim(out, local, me, axis=0)
    ahead = n // 2
    behind = n - 1 - ahead
    moving_next = local
    moving_prev = local
    for step in range(1, ahead + 1):
        moving_next = lax.ppermute(moving_next, axis, to_next)
        source = jnp.asarray([order[(where[d] - step) % n] for d in range(n)], jnp.int32)[me]
        out = lax.dynamic_update_index_in_dim(out, moving_next, source, axis=0)
        if step <= behind:
            moving_prev = lax.ppermute(moving_prev, axis, to_prev)
            source = jnp.asarray([order[(where[d] + step) % n] for d in range(n)], jnp.int32)[me]
            out = lax.dynamic_update_index_in_dim(out, moving_prev, source, axis=0)
    return out.reshape((n * rows,) + local.shape[1:])


def ring_reduce_scatter(full, axis):
    n = lax.axis_size(axis)
    rows = full.shape[0] // n
    if n > 16:
        return lax.psum_scatter(
            full.astype(jnp.bfloat16), axis, scatter_dimension=0, tiled=True
        ).astype(jnp.float32)
    order, where, to_next, to_prev = ring_tables(n)
    me = lax.axis_index(axis)

    def chunk(shift):
        index = jnp.asarray([order[(where[d] + shift) % n] for d in range(n)], jnp.int32)[me]
        return lax.dynamic_slice_in_dim(full, index * rows, rows, axis=0)

    ahead = n // 2
    behind = n - 1 - ahead
    part_next = None
    part_prev = None
    for step in range(ahead):
        mine = chunk(ahead - step)
        part_next = mine if part_next is None else part_next.astype(jnp.float32) + mine
        part_next = lax.ppermute(part_next.astype(jnp.bfloat16), axis, to_next)
        if step < behind:
            mine = chunk(step - behind)
            part_prev = mine if part_prev is None else part_prev.astype(jnp.float32) + mine
            part_prev = lax.ppermute(part_prev.astype(jnp.bfloat16), axis, to_prev)
    total = lax.dynamic_slice_in_dim(full, me * rows, rows, axis=0) + part_next.astype(jnp.float32)
    if part_prev is not None:
        total = total + part_prev.astype(jnp.float32)
    return total


def tensor_sum(term, axis):
    n = lax.axis_size(axis)
    if n != 4:
        return lax.psum(term, axis).astype(jnp.float32)
    half = term.shape[0] // 2
    me = lax.axis_index(axis)
    core = me % 2
    keep = lax.dynamic_slice_in_dim(term, core * half, half, axis=0)
    give = lax.dynamic_slice_in_dim(term, (1 - core) * half, half, axis=0)
    on_chip = [(i, i ^ 1) for i in range(n)]
    across = [(i, i ^ 2) for i in range(n)]
    mine = keep.astype(jnp.float32) + lax.ppermute(give, axis, on_chip).astype(jnp.float32)
    total = mine + lax.ppermute(mine.astype(term.dtype), axis, across).astype(jnp.float32)
    back = lax.ppermute(total.astype(term.dtype), axis, on_chip).astype(jnp.float32)
    first = jnp.where(core == 0, total, back)
    second = jnp.where(core == 0, back, total)
    return jnp.concatenate([first, second], axis=0)


def on_device(
    tokens,
    piece_starts,
    attn_gain,
    w_query,
    w_key,
    w_value,
    w_outgate,
    w_forget,
    forget_bias,
    w_output,
    ffn_gain,
    w_gate,
    w_up,
    w_down,
    cotangent,
):
    sequences, length, width = tokens.shape
    heads_here = w_forget.shape[1]
    share_width = w_query.shape[1]
    head_size = share_width // heads_here
    row_count = sequences * length
    block = w_query.shape[0]
    units = w_gate.shape[1]

    def head_view(values):
        return values.reshape(sequences, length, heads_here, head_size)

    attn_local = jnp.concatenate(
        [w_output.T, w_query, w_key, w_value, w_outgate, w_forget, attn_gain[:, None]], axis=1
    )
    attn_full = lax.all_gather(attn_local, "dp", axis=0, tiled=True)
    ffn_local = jnp.concatenate([w_gate, w_up, w_down.T, ffn_gain[:, None]], axis=1)
    ffn_local, attn_full = lax.optimization_barrier((ffn_local, attn_full))
    output_t = attn_full[:, :share_width]
    joined = attn_full[:, share_width : 5 * share_width]
    joined_five = attn_full[:, share_width : 5 * share_width + heads_here]
    forget_w = attn_full[:, 5 * share_width : 5 * share_width + heads_here]
    gain_one = attn_full[:, 5 * share_width + heads_here].astype(jnp.float32)
    ffn_full = lax.all_gather(ffn_local, "dp", axis=0, tiled=True)
    gate_up_w = ffn_full[:, : 2 * units]
    down_t = ffn_full[:, 2 * units : 3 * units]
    gain_two = ffn_full[:, 3 * units].astype(jnp.float32)

    inputs = tokens.reshape(row_count, width).astype(jnp.float32)
    scale_one = lax.rsqrt(jnp.mean(inputs * inputs, axis=-1, keepdims=True) + epsilon)
    unit_one = inputs * scale_one
    normed = (unit_one * gain_one).astype(jnp.bfloat16)
    projected = project(normed, joined)
    query_all = head_view(projected[:, :share_width].astype(jnp.bfloat16))
    key_all = head_view(projected[:, share_width : 2 * share_width].astype(jnp.bfloat16))
    value_all = head_view(projected[:, 2 * share_width : 3 * share_width].astype(jnp.bfloat16))
    gate_pre = projected[:, 3 * share_width :]
    forget_pre = project(normed, forget_w) + forget_bias[None, :]
    log_forget = jax.nn.log_sigmoid(forget_pre).reshape(sequences, length, heads_here)
    attended, normalizer = lax.map(
        attend_forward, (query_all, key_all, value_all, log_forget, piece_starts)
    )
    attended_flat = attended.reshape(row_count, share_width)
    gate_open = jax.nn.sigmoid(gate_pre)
    gated = (attended_flat * gate_open).astype(jnp.bfloat16)
    attention = tensor_sum(contract_cols(gated, output_t).astype(jnp.bfloat16), "tensor")
    hidden = inputs + attention
    scale_two = lax.rsqrt(jnp.mean(hidden * hidden, axis=-1, keepdims=True) + epsilon)
    unit_two = hidden * scale_two
    normed_two = (unit_two * gain_two).astype(jnp.bfloat16)
    inner_pre = project(normed_two, gate_up_w)
    gate_part = inner_pre[:, :units]
    up_part = inner_pre[:, units:]
    inner = (jax.nn.silu(gate_part) * up_part).astype(jnp.bfloat16)
    ffn_term = contract_cols(inner, down_t).astype(jnp.bfloat16)
    upstream_low = cotangent.reshape(row_count, width)
    upstream = upstream_low.astype(jnp.float32)
    grad_inner = project(upstream_low, down_t)
    sigma = jax.nn.sigmoid(gate_part)
    grad_gate = (grad_inner * up_part * sigma * (1.0 + gate_part * (1.0 - sigma))).astype(
        jnp.bfloat16
    )
    grad_up = (grad_inner * gate_part * sigma).astype(jnp.bfloat16)
    grad_gate_up = jnp.concatenate([grad_gate, grad_up], axis=1)
    grad_normed_two = tensor_sum(
        contract_cols(grad_gate_up, gate_up_w).astype(jnp.bfloat16), "tensor"
    )
    ffn_term, grad_normed_two = lax.optimization_barrier((ffn_term, grad_normed_two))
    ffn_out = tensor_sum(ffn_term, "tensor")
    grad_down_t = contract_rows(upstream_low, inner)
    grad_gate_up_w = contract_rows(normed_two, grad_gate_up)
    grad_ffn_gain = jnp.sum(grad_normed_two * unit_two, axis=0)
    grad_unit_two = grad_normed_two * gain_two
    grad_hidden = upstream + scale_two * (
        grad_unit_two - unit_two * jnp.mean(grad_unit_two * unit_two, axis=-1, keepdims=True)
    )
    hidden_low = grad_hidden.astype(jnp.bfloat16)
    grad_output_t = contract_rows(hidden_low, gated)
    early_grads = jnp.concatenate(
        [grad_gate_up_w, grad_down_t, grad_output_t, grad_ffn_gain[:, None]], axis=1
    )
    early_grads, hidden_low = lax.optimization_barrier((early_grads, hidden_low))
    early_sums = lax.psum_scatter(
        early_grads.astype(jnp.bfloat16), "dp", scatter_dimension=0, tiled=True
    ).astype(jnp.float32)
    grad_gated = project(hidden_low, output_t)
    grad_attended = (grad_gated * gate_open).astype(jnp.bfloat16)
    grad_gate_pre = (grad_gated * attended_flat * gate_open * (1.0 - gate_open)).astype(
        jnp.bfloat16
    )
    grad_query, grad_key, grad_value, grad_log = lax.map(
        attend_backward,
        (
            query_all,
            key_all,
            value_all,
            log_forget,
            piece_starts,
            attended,
            normalizer,
            head_view(grad_attended),
        ),
    )
    grad_forget = (grad_log.reshape(row_count, heads_here) * jax.nn.sigmoid(-forget_pre)).astype(
        jnp.bfloat16
    )
    grad_five = jnp.concatenate(
        [
            grad_query.reshape(row_count, share_width),
            grad_key.reshape(row_count, share_width),
            grad_value.reshape(row_count, share_width),
            grad_gate_pre,
            grad_forget,
        ],
        axis=1,
    )
    ffn_out, grad_five = lax.optimization_barrier((ffn_out, grad_five))
    output = (hidden + ffn_out).astype(jnp.bfloat16).reshape(tokens.shape)
    grad_bias = jnp.sum(grad_forget.astype(jnp.float32), axis=0)
    place = jnp.arange(width, dtype=jnp.int32) % block
    bias_col = jnp.where(
        place < heads_here, jnp.take(grad_bias, jnp.minimum(place, heads_here - 1)), 0.0
    )
    late_grads = contract_rows(normed, grad_five)
    grad_normed = tensor_sum(contract_cols(grad_five, joined_five).astype(jnp.bfloat16), "tensor")
    grad_attn_gain = jnp.sum(grad_normed * unit_one, axis=0)
    late_sums = ring_reduce_scatter(
        jnp.concatenate([late_grads, bias_col[:, None], grad_attn_gain[:, None]], axis=1), "dp"
    )
    grad_unit_one = grad_normed * gain_one
    grad_inputs = grad_hidden + scale_one * (
        grad_unit_one - unit_one * jnp.mean(grad_unit_one * unit_one, axis=-1, keepdims=True)
    )
    tokens_grad = grad_inputs.astype(jnp.bfloat16).reshape(tokens.shape)
    forget_at = 4 * share_width
    return (
        output,
        tokens_grad,
        late_sums[:, forget_at + heads_here + 1],
        late_sums[:, :share_width],
        late_sums[:, share_width : 2 * share_width],
        late_sums[:, 2 * share_width : 3 * share_width],
        late_sums[:, 3 * share_width : 4 * share_width],
        late_sums[:, forget_at : forget_at + heads_here],
        late_sums[:heads_here, forget_at + heads_here],
        early_sums[:, 3 * units : 3 * units + share_width].T,
        early_sums[:, 3 * units + share_width],
        early_sums[:, :units],
        early_sums[:, units : 2 * units],
        early_sums[:, 2 * units : 3 * units].T,
    )


def solution(mesh):
    placed = (
        P("dp", None, None),
        P("dp", None),
        P("dp"),
        P("dp", "tensor"),
        P("dp", "tensor"),
        P("dp", "tensor"),
        P("dp", "tensor"),
        P("dp", "tensor"),
        P("tensor"),
        P("tensor", "dp"),
        P("dp"),
        P("dp", "tensor"),
        P("dp", "tensor"),
        P("tensor", "dp"),
        P("dp", None, None),
    )
    return jax.shard_map(
        on_device,
        mesh=mesh,
        in_specs=placed,
        out_specs=(
            P("dp", None, None),
            P("dp", None, None),
            P("dp"),
            P("dp", "tensor"),
            P("dp", "tensor"),
            P("dp", "tensor"),
            P("dp", "tensor"),
            P("dp", "tensor"),
            P("tensor"),
            P("tensor", "dp"),
            P("dp"),
            P("dp", "tensor"),
            P("dp", "tensor"),
            P("tensor", "dp"),
        ),
        check_vma=False,
    )
```

```python
import jax
import jax.numpy as jnp
from jax import lax
from jax.sharding import PartitionSpec as P

PIECE = 256


epsilon = 1e-06
masked_value = -1e30


def project(left, right):
    return jnp.dot(left, right, preferred_element_type=jnp.float32)


def contract_rows(left, right):
    return lax.dot_general(
        left, right, (((0,), (0,)), ((), ())), preferred_element_type=jnp.float32
    )


def contract_cols(left, right):
    return lax.dot_general(
        left, right, (((1,), (1,)), ((), ())), preferred_element_type=jnp.float32
    )


def allowed_pairs(starts, length):
    places = jnp.arange(length, dtype=jnp.int32)
    inside = (
        (starts[:, None] >= 0)
        & (places[None, :] >= starts[:, None])
        & (places[None, :] < starts[:, None] + PIECE)
    )
    labels = jnp.sum(
        jnp.where(inside, jnp.arange(1, starts.shape[0] + 1, dtype=jnp.int32)[:, None], 0), axis=0
    )
    same = (labels[:, None] == labels[None, :]) & (labels[:, None] > 0)
    return (places[None, :] <= places[:, None]) | same


def key_reach(first_row, block_rows, length, slots):
    width = length // slots
    return min(length, -(-(first_row + block_rows) // width) * width)


def block_scores(query_rows, key_all, decay, allowed_rows, first_row):
    count = query_rows.shape[0]
    reach = key_all.shape[0]
    raw = jnp.einsum(
        "qhd,khd->hqk", query_rows, key_all, preferred_element_type=jnp.float32
    ) * query_rows.shape[-1] ** (-0.5)
    apart = (
        lax.slice_in_dim(decay, first_row, first_row + count, axis=1)[:, :, None]
        - decay[:, None, :reach]
    )
    return (jnp.where(allowed_rows[None], raw - jnp.abs(apart), masked_value), apart)


def attend_forward(items):
    query_all, key_all, value_all, log_forget, starts = items
    length = query_all.shape[0]
    block_rows = min(512, length)
    decay = jnp.cumsum(log_forget, axis=0).T
    allowed = allowed_pairs(starts, length)
    results = []
    normalizers = []
    for first_row in range(0, length, block_rows):
        reach = key_reach(first_row, block_rows, length, starts.shape[0])
        scores, apart = block_scores(
            query_all[first_row : first_row + block_rows],
            key_all[:reach],
            decay,
            allowed[first_row : first_row + block_rows, :reach],
            first_row,
        )
        largest = jnp.max(scores, axis=-1, keepdims=True)
        weights = jnp.exp(scores - largest)
        denominator = jnp.sum(weights, axis=-1, keepdims=True)
        chances = (weights / denominator).astype(jnp.bfloat16)
        results.append(
            jnp.einsum(
                "hqk,khd->qhd", chances, value_all[:reach], preferred_element_type=jnp.float32
            )
        )
        normalizers.append(largest + jnp.log(denominator))
    return (jnp.concatenate(results, axis=0), jnp.concatenate(normalizers, axis=1))


def attend_backward(items):
    query_all, key_all, value_all, log_forget, starts, attended, normalizer, grad_out = items
    length = query_all.shape[0]
    block_rows = min(512, length)
    scale = query_all.shape[-1] ** (-0.5)
    decay = jnp.cumsum(log_forget, axis=0).T
    allowed = allowed_pairs(starts, length)
    grad_key = jnp.zeros(key_all.shape, jnp.float32)
    grad_value = jnp.zeros(value_all.shape, jnp.float32)
    grad_decay = jnp.zeros(decay.shape, jnp.float32)
    query_parts = []
    row_parts = []
    for first_row in range(0, length, block_rows):
        reach = key_reach(first_row, block_rows, length, starts.shape[0])
        key_rows = key_all[:reach]
        value_rows = value_all[:reach]
        query_rows = query_all[first_row : first_row + block_rows]
        out_rows = grad_out[first_row : first_row + block_rows]
        scores, apart = block_scores(
            query_rows, key_rows, decay, allowed[first_row : first_row + block_rows, :reach],
            first_row,
        )
        chances = jnp.exp(scores - normalizer[:, first_row : first_row + block_rows])
        grad_chance = jnp.einsum(
            "qhd,khd->hqk", out_rows, value_rows, preferred_element_type=jnp.float32
        )
        offset = jnp.sum(
            out_rows.astype(jnp.float32) * attended[first_row : first_row + block_rows], axis=-1
        ).T[:, :, None]
        grad_score = chances * (grad_chance - offset)
        grad_rounded = grad_score.astype(jnp.bfloat16)
        grad_value = grad_value.at[:reach].add(
            jnp.einsum(
                "hqk,qhd->khd",
                chances.astype(jnp.bfloat16),
                out_rows,
                preferred_element_type=jnp.float32,
            )
        )
        grad_key = grad_key.at[:reach].add(
            jnp.einsum(
                "hqk,qhd->khd", grad_rounded, query_rows, preferred_element_type=jnp.float32
            )
            * scale
        )
        query_parts.append(
            jnp.einsum("hqk,khd->qhd", grad_rounded, key_rows, preferred_element_type=jnp.float32)
            * scale
        )
        signed = grad_score * jnp.sign(apart)
        grad_decay = grad_decay.at[:, :reach].add(jnp.sum(signed, axis=1))
        row_parts.append(-jnp.sum(signed, axis=-1))
    grad_decay = grad_decay + jnp.concatenate(row_parts, axis=1)
    grad_log = jnp.flip(jnp.cumsum(jnp.flip(grad_decay, axis=1), axis=1), axis=1).T
    grad_query = jnp.concatenate(query_parts, axis=0)
    return (
        grad_query.astype(jnp.bfloat16),
        grad_key.astype(jnp.bfloat16),
        grad_value.astype(jnp.bfloat16),
        grad_log,
    )


def ring_order(n):
    inner = 2 if n % 2 == 0 else 1
    outer = n // inner
    order = [o * inner for o in range(outer)]
    if inner == 2:
        order += [o * inner + 1 for o in reversed(range(outer))]
    return order


def ring_tables(n):
    order = ring_order(n)
    where = [0] * n
    for p, d in enumerate(order):
        where[d] = p
    to_next = [(order[p], order[(p + 1) % n]) for p in range(n)]
    to_prev = [(order[p], order[(p - 1) % n]) for p in range(n)]
    return order, where, to_next, to_prev


def ring_gather(local, axis):
    n = lax.axis_size(axis)
    rows = local.shape[0]
    if n > 16:
        return lax.all_gather(local, axis, axis=0, tiled=True)
    order, where, to_next, to_prev = ring_tables(n)
    me = lax.axis_index(axis)
    out = jnp.zeros((n, rows) + local.shape[1:], local.dtype)
    out = lax.dynamic_update_index_in_dim(out, local, me, axis=0)
    ahead = n // 2
    behind = n - 1 - ahead
    moving_next = local
    moving_prev = local
    for step in range(1, ahead + 1):
        moving_next = lax.ppermute(moving_next, axis, to_next)
        source = jnp.asarray([order[(where[d] - step) % n] for d in range(n)], jnp.int32)[me]
        out = lax.dynamic_update_index_in_dim(out, moving_next, source, axis=0)
        if step <= behind:
            moving_prev = lax.ppermute(moving_prev, axis, to_prev)
            source = jnp.asarray([order[(where[d] + step) % n] for d in range(n)], jnp.int32)[me]
            out = lax.dynamic_update_index_in_dim(out, moving_prev, source, axis=0)
    return out.reshape((n * rows,) + local.shape[1:])


def ring_reduce_scatter(full, axis):
    n = lax.axis_size(axis)
    rows = full.shape[0] // n
    if n > 16:
        return lax.psum_scatter(
            full.astype(jnp.bfloat16), axis, scatter_dimension=0, tiled=True
        ).astype(jnp.float32)
    order, where, to_next, to_prev = ring_tables(n)
    me = lax.axis_index(axis)

    def chunk(shift):
        index = jnp.asarray([order[(where[d] + shift) % n] for d in range(n)], jnp.int32)[me]
        return lax.dynamic_slice_in_dim(full, index * rows, rows, axis=0)

    ahead = n // 2
    behind = n - 1 - ahead
    part_next = None
    part_prev = None
    for step in range(ahead):
        mine = chunk(ahead - step)
        part_next = mine if part_next is None else part_next.astype(jnp.float32) + mine
        part_next = lax.ppermute(part_next.astype(jnp.bfloat16), axis, to_next)
        if step < behind:
            mine = chunk(step - behind)
            part_prev = mine if part_prev is None else part_prev.astype(jnp.float32) + mine
            part_prev = lax.ppermute(part_prev.astype(jnp.bfloat16), axis, to_prev)
    total = lax.dynamic_slice_in_dim(full, me * rows, rows, axis=0) + part_next.astype(jnp.float32)
    if part_prev is not None:
        total = total + part_prev.astype(jnp.float32)
    return total


def tensor_sum(term, axis):
    n = lax.axis_size(axis)
    if n != 4:
        return lax.psum(term, axis).astype(jnp.float32)
    half = term.shape[0] // 2
    me = lax.axis_index(axis)
    core = me % 2
    keep = lax.dynamic_slice_in_dim(term, core * half, half, axis=0)
    give = lax.dynamic_slice_in_dim(term, (1 - core) * half, half, axis=0)
    on_chip = [(i, i ^ 1) for i in range(n)]
    across = [(i, i ^ 2) for i in range(n)]
    mine = keep.astype(jnp.float32) + lax.ppermute(give, axis, on_chip).astype(jnp.float32)
    total = mine + lax.ppermute(mine.astype(term.dtype), axis, across).astype(jnp.float32)
    back = lax.ppermute(total.astype(term.dtype), axis, on_chip).astype(jnp.float32)
    first = jnp.where(core == 0, total, back)
    second = jnp.where(core == 0, back, total)
    return jnp.concatenate([first, second], axis=0)


def on_device(
    tokens,
    piece_starts,
    attn_gain,
    w_query,
    w_key,
    w_value,
    w_outgate,
    w_forget,
    forget_bias,
    w_output,
    ffn_gain,
    w_gate,
    w_up,
    w_down,
    cotangent,
):
    sequences, length, width = tokens.shape
    heads_here = w_forget.shape[1]
    share_width = w_query.shape[1]
    head_size = share_width // heads_here
    row_count = sequences * length
    block = w_query.shape[0]
    units = w_gate.shape[1]

    def head_view(values):
        return values.reshape(sequences, length, heads_here, head_size)

    attn_local = jnp.concatenate(
        [w_output.T, w_query, w_key, w_value, w_outgate, w_forget, attn_gain[:, None]], axis=1
    )
    attn_full = lax.all_gather(attn_local, "dp", axis=0, tiled=True)
    ffn_local = jnp.concatenate([w_gate, w_up, w_down.T, ffn_gain[:, None]], axis=1)
    ffn_local, attn_full = lax.optimization_barrier((ffn_local, attn_full))
    output_t = attn_full[:, :share_width]
    joined = attn_full[:, share_width : 5 * share_width]
    joined_five = attn_full[:, share_width : 5 * share_width + heads_here]
    forget_w = attn_full[:, 5 * share_width : 5 * share_width + heads_here]
    gain_one = attn_full[:, 5 * share_width + heads_here].astype(jnp.float32)
    ffn_full = lax.all_gather(ffn_local, "dp", axis=0, tiled=True)
    gate_up_w = ffn_full[:, : 2 * units]
    down_t = ffn_full[:, 2 * units : 3 * units]
    gain_two = ffn_full[:, 3 * units].astype(jnp.float32)

    inputs = tokens.reshape(row_count, width).astype(jnp.float32)
    scale_one = lax.rsqrt(jnp.mean(inputs * inputs, axis=-1, keepdims=True) + epsilon)
    unit_one = inputs * scale_one
    normed = (unit_one * gain_one).astype(jnp.bfloat16)
    projected = project(normed, joined)
    query_all = head_view(projected[:, :share_width].astype(jnp.bfloat16))
    key_all = head_view(projected[:, share_width : 2 * share_width].astype(jnp.bfloat16))
    value_all = head_view(projected[:, 2 * share_width : 3 * share_width].astype(jnp.bfloat16))
    gate_pre = projected[:, 3 * share_width :]
    forget_pre = project(normed, forget_w) + forget_bias[None, :]
    log_forget = jax.nn.log_sigmoid(forget_pre).reshape(sequences, length, heads_here)
    attended, normalizer = lax.map(
        attend_forward, (query_all, key_all, value_all, log_forget, piece_starts)
    )
    attended_flat = attended.reshape(row_count, share_width)
    gate_open = jax.nn.sigmoid(gate_pre)
    gated = (attended_flat * gate_open).astype(jnp.bfloat16)
    attention = tensor_sum(contract_cols(gated, output_t).astype(jnp.bfloat16), "tensor")
    hidden = inputs + attention
    scale_two = lax.rsqrt(jnp.mean(hidden * hidden, axis=-1, keepdims=True) + epsilon)
    unit_two = hidden * scale_two
    normed_two = (unit_two * gain_two).astype(jnp.bfloat16)
    inner_pre = project(normed_two, gate_up_w)
    gate_part = inner_pre[:, :units]
    up_part = inner_pre[:, units:]
    inner = (jax.nn.silu(gate_part) * up_part).astype(jnp.bfloat16)
    ffn_term = contract_cols(inner, down_t).astype(jnp.bfloat16)
    upstream_low = cotangent.reshape(row_count, width)
    upstream = upstream_low.astype(jnp.float32)
    grad_inner = project(upstream_low, down_t)
    sigma = jax.nn.sigmoid(gate_part)
    grad_gate = (grad_inner * up_part * sigma * (1.0 + gate_part * (1.0 - sigma))).astype(
        jnp.bfloat16
    )
    grad_up = (grad_inner * gate_part * sigma).astype(jnp.bfloat16)
    grad_gate_up = jnp.concatenate([grad_gate, grad_up], axis=1)
    grad_down_t = contract_rows(upstream_low, inner)
    grad_gate_up_w = contract_rows(normed_two, grad_gate_up)
    ffn_grads = jnp.concatenate([grad_gate_up_w, grad_down_t], axis=1).astype(jnp.bfloat16)
    grad_normed_two = tensor_sum(
        contract_cols(grad_gate_up, gate_up_w).astype(jnp.bfloat16), "tensor"
    )
    ffn_grads, grad_normed_two = lax.optimization_barrier((ffn_grads, grad_normed_two))
    ffn_sums = lax.psum_scatter(ffn_grads, "dp", scatter_dimension=0, tiled=True).astype(
        jnp.float32
    )
    ffn_term, grad_normed_two = lax.optimization_barrier((ffn_term, grad_normed_two))
    ffn_out = tensor_sum(ffn_term, "tensor")
    grad_ffn_gain = jnp.sum(grad_normed_two * unit_two, axis=0)
    grad_unit_two = grad_normed_two * gain_two
    grad_hidden = upstream + scale_two * (
        grad_unit_two - unit_two * jnp.mean(grad_unit_two * unit_two, axis=-1, keepdims=True)
    )
    hidden_low = grad_hidden.astype(jnp.bfloat16)
    grad_output_t = contract_rows(hidden_low, gated)
    grad_gated = project(hidden_low, output_t)
    grad_attended = (grad_gated * gate_open).astype(jnp.bfloat16)
    grad_gate_pre = (grad_gated * attended_flat * gate_open * (1.0 - gate_open)).astype(
        jnp.bfloat16
    )
    grad_query, grad_key, grad_value, grad_log = lax.map(
        attend_backward,
        (
            query_all,
            key_all,
            value_all,
            log_forget,
            piece_starts,
            attended,
            normalizer,
            head_view(grad_attended),
        ),
    )
    grad_forget = (grad_log.reshape(row_count, heads_here) * jax.nn.sigmoid(-forget_pre)).astype(
        jnp.bfloat16
    )
    grad_five = jnp.concatenate(
        [
            grad_query.reshape(row_count, share_width),
            grad_key.reshape(row_count, share_width),
            grad_value.reshape(row_count, share_width),
            grad_gate_pre,
            grad_forget,
        ],
        axis=1,
    )
    ffn_out, grad_five = lax.optimization_barrier((ffn_out, grad_five))
    output = (hidden + ffn_out).astype(jnp.bfloat16).reshape(tokens.shape)
    grad_bias = jnp.sum(grad_forget.astype(jnp.float32), axis=0)
    place = jnp.arange(width, dtype=jnp.int32) % block
    bias_col = jnp.where(
        place < heads_here, jnp.take(grad_bias, jnp.minimum(place, heads_here - 1)), 0.0
    )
    late_grads = contract_rows(normed, grad_five)
    grad_normed = tensor_sum(contract_cols(grad_five, joined_five).astype(jnp.bfloat16), "tensor")
    grad_attn_gain = jnp.sum(grad_normed * unit_one, axis=0)
    late_sums = ring_reduce_scatter(
        jnp.concatenate(
            [
                late_grads,
                bias_col[:, None],
                grad_attn_gain[:, None],
                grad_ffn_gain[:, None],
                grad_output_t,
            ],
            axis=1,
        ),
        "dp",
    )
    out_at = 4 * share_width + heads_here + 3
    grad_unit_one = grad_normed * gain_one
    grad_inputs = grad_hidden + scale_one * (
        grad_unit_one - unit_one * jnp.mean(grad_unit_one * unit_one, axis=-1, keepdims=True)
    )
    tokens_grad = grad_inputs.astype(jnp.bfloat16).reshape(tokens.shape)
    forget_at = 4 * share_width
    return (
        output,
        tokens_grad,
        late_sums[:, forget_at + heads_here + 1],
        late_sums[:, :share_width],
        late_sums[:, share_width : 2 * share_width],
        late_sums[:, 2 * share_width : 3 * share_width],
        late_sums[:, 3 * share_width : 4 * share_width],
        late_sums[:, forget_at : forget_at + heads_here],
        late_sums[:heads_here, forget_at + heads_here],
        late_sums[:, out_at : out_at + share_width].T,
        late_sums[:, out_at - 1],
        ffn_sums[:, :units],
        ffn_sums[:, units : 2 * units],
        ffn_sums[:, 2 * units : 3 * units].T,
    )


def solution(mesh):
    placed = (
        P("dp", None, None),
        P("dp", None),
        P("dp"),
        P("dp", "tensor"),
        P("dp", "tensor"),
        P("dp", "tensor"),
        P("dp", "tensor"),
        P("dp", "tensor"),
        P("tensor"),
        P("tensor", "dp"),
        P("dp"),
        P("dp", "tensor"),
        P("dp", "tensor"),
        P("tensor", "dp"),
        P("dp", None, None),
    )
    return jax.shard_map(
        on_device,
        mesh=mesh,
        in_specs=placed,
        out_specs=(
            P("dp", None, None),
            P("dp", None, None),
            P("dp"),
            P("dp", "tensor"),
            P("dp", "tensor"),
            P("dp", "tensor"),
            P("dp", "tensor"),
            P("dp", "tensor"),
            P("tensor"),
            P("tensor", "dp"),
            P("dp"),
            P("dp", "tensor"),
            P("dp", "tensor"),
            P("tensor", "dp"),
        ),
        check_vma=False,
    )
```

```python
import jax
import jax.numpy as jnp
from jax import lax
from jax.sharding import PartitionSpec as P

PIECE = 256


epsilon = 1e-06
masked_value = -1e30


def project(left, right):
    return jnp.dot(left, right, preferred_element_type=jnp.float32)


def contract_rows(left, right):
    return lax.dot_general(
        left, right, (((0,), (0,)), ((), ())), preferred_element_type=jnp.float32
    )


def contract_cols(left, right):
    return lax.dot_general(
        left, right, (((1,), (1,)), ((), ())), preferred_element_type=jnp.float32
    )


def allowed_pairs(starts, length):
    places = jnp.arange(length, dtype=jnp.int32)
    inside = (
        (starts[:, None] >= 0)
        & (places[None, :] >= starts[:, None])
        & (places[None, :] < starts[:, None] + PIECE)
    )
    labels = jnp.sum(
        jnp.where(inside, jnp.arange(1, starts.shape[0] + 1, dtype=jnp.int32)[:, None], 0), axis=0
    )
    same = (labels[:, None] == labels[None, :]) & (labels[:, None] > 0)
    return (places[None, :] <= places[:, None]) | same


def key_reach(first_row, block_rows, length, slots):
    width = length // slots
    return min(length, -(-(first_row + block_rows) // width) * width)


def block_scores(query_rows, key_all, decay, allowed_rows, first_row):
    count = query_rows.shape[0]
    reach = key_all.shape[0]
    raw = jnp.einsum(
        "qhd,khd->hqk", query_rows, key_all, preferred_element_type=jnp.float32
    ) * query_rows.shape[-1] ** (-0.5)
    apart = (
        lax.slice_in_dim(decay, first_row, first_row + count, axis=1)[:, :, None]
        - decay[:, None, :reach]
    )
    return (jnp.where(allowed_rows[None], raw - jnp.abs(apart), masked_value), apart)


def attend_forward(items):
    query_all, key_all, value_all, log_forget, starts = items
    length = query_all.shape[0]
    block_rows = min(512, length)
    decay = jnp.cumsum(log_forget, axis=0).T
    allowed = allowed_pairs(starts, length)
    results = []
    normalizers = []
    for first_row in range(0, length, block_rows):
        reach = key_reach(first_row, block_rows, length, starts.shape[0])
        scores, apart = block_scores(
            query_all[first_row : first_row + block_rows],
            key_all[:reach],
            decay,
            allowed[first_row : first_row + block_rows, :reach],
            first_row,
        )
        largest = jnp.max(scores, axis=-1, keepdims=True)
        weights = jnp.exp(scores - largest)
        denominator = jnp.sum(weights, axis=-1, keepdims=True)
        chances = (weights / denominator).astype(jnp.bfloat16)
        results.append(
            jnp.einsum(
                "hqk,khd->qhd", chances, value_all[:reach], preferred_element_type=jnp.float32
            )
        )
        normalizers.append(largest + jnp.log(denominator))
    return (jnp.concatenate(results, axis=0), jnp.concatenate(normalizers, axis=1))


def attend_backward(items):
    query_all, key_all, value_all, log_forget, starts, attended, normalizer, grad_out = items
    length = query_all.shape[0]
    block_rows = min(512, length)
    scale = query_all.shape[-1] ** (-0.5)
    decay = jnp.cumsum(log_forget, axis=0).T
    allowed = allowed_pairs(starts, length)
    grad_key = jnp.zeros(key_all.shape, jnp.float32)
    grad_value = jnp.zeros(value_all.shape, jnp.float32)
    grad_decay = jnp.zeros(decay.shape, jnp.float32)
    query_parts = []
    row_parts = []
    for first_row in range(0, length, block_rows):
        reach = key_reach(first_row, block_rows, length, starts.shape[0])
        key_rows = key_all[:reach]
        value_rows = value_all[:reach]
        query_rows = query_all[first_row : first_row + block_rows]
        out_rows = grad_out[first_row : first_row + block_rows]
        scores, apart = block_scores(
            query_rows, key_rows, decay, allowed[first_row : first_row + block_rows, :reach],
            first_row,
        )
        chances = jnp.exp(scores - normalizer[:, first_row : first_row + block_rows])
        grad_chance = jnp.einsum(
            "qhd,khd->hqk", out_rows, value_rows, preferred_element_type=jnp.float32
        )
        offset = jnp.sum(
            out_rows.astype(jnp.float32) * attended[first_row : first_row + block_rows], axis=-1
        ).T[:, :, None]
        grad_score = chances * (grad_chance - offset)
        grad_rounded = grad_score.astype(jnp.bfloat16)
        grad_value = grad_value.at[:reach].add(
            jnp.einsum(
                "hqk,qhd->khd",
                chances.astype(jnp.bfloat16),
                out_rows,
                preferred_element_type=jnp.float32,
            )
        )
        grad_key = grad_key.at[:reach].add(
            jnp.einsum(
                "hqk,qhd->khd", grad_rounded, query_rows, preferred_element_type=jnp.float32
            )
            * scale
        )
        query_parts.append(
            jnp.einsum("hqk,khd->qhd", grad_rounded, key_rows, preferred_element_type=jnp.float32)
            * scale
        )
        signed = grad_score * jnp.sign(apart)
        grad_decay = grad_decay.at[:, :reach].add(jnp.sum(signed, axis=1))
        row_parts.append(-jnp.sum(signed, axis=-1))
    grad_decay = grad_decay + jnp.concatenate(row_parts, axis=1)
    grad_log = jnp.flip(jnp.cumsum(jnp.flip(grad_decay, axis=1), axis=1), axis=1).T
    grad_query = jnp.concatenate(query_parts, axis=0)
    return (
        grad_query.astype(jnp.bfloat16),
        grad_key.astype(jnp.bfloat16),
        grad_value.astype(jnp.bfloat16),
        grad_log,
    )


def ring_order(n):
    inner = 2 if n % 2 == 0 else 1
    outer = n // inner
    order = [o * inner for o in range(outer)]
    if inner == 2:
        order += [o * inner + 1 for o in reversed(range(outer))]
    return order


def ring_tables(n):
    order = ring_order(n)
    where = [0] * n
    for p, d in enumerate(order):
        where[d] = p
    to_next = [(order[p], order[(p + 1) % n]) for p in range(n)]
    to_prev = [(order[p], order[(p - 1) % n]) for p in range(n)]
    return order, where, to_next, to_prev


def ring_gather(local, axis):
    n = lax.axis_size(axis)
    rows = local.shape[0]
    if n > 16:
        return lax.all_gather(local, axis, axis=0, tiled=True)
    order, where, to_next, to_prev = ring_tables(n)
    me = lax.axis_index(axis)
    out = jnp.zeros((n, rows) + local.shape[1:], local.dtype)
    out = lax.dynamic_update_index_in_dim(out, local, me, axis=0)
    ahead = n // 2
    behind = n - 1 - ahead
    moving_next = local
    moving_prev = local
    for step in range(1, ahead + 1):
        moving_next = lax.ppermute(moving_next, axis, to_next)
        source = jnp.asarray([order[(where[d] - step) % n] for d in range(n)], jnp.int32)[me]
        out = lax.dynamic_update_index_in_dim(out, moving_next, source, axis=0)
        if step <= behind:
            moving_prev = lax.ppermute(moving_prev, axis, to_prev)
            source = jnp.asarray([order[(where[d] + step) % n] for d in range(n)], jnp.int32)[me]
            out = lax.dynamic_update_index_in_dim(out, moving_prev, source, axis=0)
    return out.reshape((n * rows,) + local.shape[1:])


def ring_reduce_scatter(full, axis):
    n = lax.axis_size(axis)
    rows = full.shape[0] // n
    if n > 16:
        return lax.psum_scatter(
            full.astype(jnp.bfloat16), axis, scatter_dimension=0, tiled=True
        ).astype(jnp.float32)
    order, where, to_next, to_prev = ring_tables(n)
    me = lax.axis_index(axis)

    def chunk(shift):
        index = jnp.asarray([order[(where[d] + shift) % n] for d in range(n)], jnp.int32)[me]
        return lax.dynamic_slice_in_dim(full, index * rows, rows, axis=0)

    ahead = n // 2
    behind = n - 1 - ahead
    part_next = None
    part_prev = None
    for step in range(ahead):
        mine = chunk(ahead - step)
        part_next = mine if part_next is None else part_next.astype(jnp.float32) + mine
        part_next = lax.ppermute(part_next.astype(jnp.bfloat16), axis, to_next)
        if step < behind:
            mine = chunk(step - behind)
            part_prev = mine if part_prev is None else part_prev.astype(jnp.float32) + mine
            part_prev = lax.ppermute(part_prev.astype(jnp.bfloat16), axis, to_prev)
    total = lax.dynamic_slice_in_dim(full, me * rows, rows, axis=0) + part_next.astype(jnp.float32)
    if part_prev is not None:
        total = total + part_prev.astype(jnp.float32)
    return total


def tensor_sum(term, axis):
    n = lax.axis_size(axis)
    if n != 4:
        return lax.psum(term, axis).astype(jnp.float32)
    half = term.shape[0] // 2
    me = lax.axis_index(axis)
    core = me % 2
    keep = lax.dynamic_slice_in_dim(term, core * half, half, axis=0)
    give = lax.dynamic_slice_in_dim(term, (1 - core) * half, half, axis=0)
    on_chip = [(i, i ^ 1) for i in range(n)]
    across = [(i, i ^ 2) for i in range(n)]
    mine = keep.astype(jnp.float32) + lax.ppermute(give, axis, on_chip).astype(jnp.float32)
    total = mine + lax.ppermute(mine.astype(term.dtype), axis, across).astype(jnp.float32)
    back = lax.ppermute(total.astype(term.dtype), axis, on_chip).astype(jnp.float32)
    first = jnp.where(core == 0, total, back)
    second = jnp.where(core == 0, back, total)
    return jnp.concatenate([first, second], axis=0)


def on_device(
    tokens,
    piece_starts,
    attn_gain,
    w_query,
    w_key,
    w_value,
    w_outgate,
    w_forget,
    forget_bias,
    w_output,
    ffn_gain,
    w_gate,
    w_up,
    w_down,
    cotangent,
):
    sequences, length, width = tokens.shape
    heads_here = w_forget.shape[1]
    share_width = w_query.shape[1]
    head_size = share_width // heads_here
    row_count = sequences * length
    block = w_query.shape[0]
    units = w_gate.shape[1]

    def head_view(values):
        return values.reshape(sequences, length, heads_here, head_size)

    attn_local = jnp.concatenate(
        [w_output.T, w_query, w_key, w_value, w_outgate, w_forget, attn_gain[:, None]], axis=1
    )
    attn_full = lax.all_gather(attn_local, "dp", axis=0, tiled=True)
    ffn_local = jnp.concatenate([w_gate, w_up, w_down.T, ffn_gain[:, None]], axis=1)
    ffn_local, attn_full = lax.optimization_barrier((ffn_local, attn_full))
    output_t = attn_full[:, :share_width]
    joined = attn_full[:, share_width : 5 * share_width]
    joined_five = attn_full[:, share_width : 5 * share_width + heads_here]
    forget_w = attn_full[:, 5 * share_width : 5 * share_width + heads_here]
    gain_one = attn_full[:, 5 * share_width + heads_here].astype(jnp.float32)
    ffn_full = lax.all_gather(ffn_local, "dp", axis=0, tiled=True)
    gate_up_w = ffn_full[:, : 2 * units]
    down_t = ffn_full[:, 2 * units : 3 * units]
    gain_two = ffn_full[:, 3 * units].astype(jnp.float32)

    inputs = tokens.reshape(row_count, width).astype(jnp.float32)
    scale_one = lax.rsqrt(jnp.mean(inputs * inputs, axis=-1, keepdims=True) + epsilon)
    unit_one = inputs * scale_one
    normed = (unit_one * gain_one).astype(jnp.bfloat16)
    projected = project(normed, joined)
    query_all = head_view(projected[:, :share_width].astype(jnp.bfloat16))
    key_all = head_view(projected[:, share_width : 2 * share_width].astype(jnp.bfloat16))
    value_all = head_view(projected[:, 2 * share_width : 3 * share_width].astype(jnp.bfloat16))
    gate_pre = projected[:, 3 * share_width :]
    forget_pre = project(normed, forget_w) + forget_bias[None, :]
    log_forget = jax.nn.log_sigmoid(forget_pre).reshape(sequences, length, heads_here)
    attended, normalizer = lax.map(
        attend_forward, (query_all, key_all, value_all, log_forget, piece_starts)
    )
    attended_flat = attended.reshape(row_count, share_width)
    gate_open = jax.nn.sigmoid(gate_pre)
    gated = (attended_flat * gate_open).astype(jnp.bfloat16)
    attention = tensor_sum(contract_cols(gated, output_t).astype(jnp.bfloat16), "tensor")
    hidden = inputs + attention
    scale_two = lax.rsqrt(jnp.mean(hidden * hidden, axis=-1, keepdims=True) + epsilon)
    unit_two = hidden * scale_two
    normed_two = (unit_two * gain_two).astype(jnp.bfloat16)
    inner_pre = project(normed_two, gate_up_w)
    gate_part = inner_pre[:, :units]
    up_part = inner_pre[:, units:]
    inner = (jax.nn.silu(gate_part) * up_part).astype(jnp.bfloat16)
    ffn_term = contract_cols(inner, down_t).astype(jnp.bfloat16)
    upstream_low = cotangent.reshape(row_count, width)
    upstream = upstream_low.astype(jnp.float32)
    grad_inner = project(upstream_low, down_t)
    sigma = jax.nn.sigmoid(gate_part)
    grad_gate = (grad_inner * up_part * sigma * (1.0 + gate_part * (1.0 - sigma))).astype(
        jnp.bfloat16
    )
    grad_up = (grad_inner * gate_part * sigma).astype(jnp.bfloat16)
    grad_gate_up = jnp.concatenate([grad_gate, grad_up], axis=1)
    grad_down_t = contract_rows(upstream_low, inner)
    grad_gate_up_w = contract_rows(normed_two, grad_gate_up)
    ffn_grads = jnp.concatenate([grad_gate_up_w, grad_down_t], axis=1).astype(jnp.bfloat16)
    grad_normed_two = tensor_sum(
        contract_cols(grad_gate_up, gate_up_w).astype(jnp.bfloat16), "tensor"
    )
    ffn_grads, grad_normed_two = lax.optimization_barrier((ffn_grads, grad_normed_two))
    ffn_sums = lax.psum_scatter(ffn_grads, "dp", scatter_dimension=0, tiled=True).astype(
        jnp.float32
    )
    ffn_term, grad_normed_two = lax.optimization_barrier((ffn_term, grad_normed_two))
    ffn_out = tensor_sum(ffn_term, "tensor")
    grad_ffn_gain = jnp.sum(grad_normed_two * unit_two, axis=0)
    grad_unit_two = grad_normed_two * gain_two
    grad_hidden = upstream + scale_two * (
        grad_unit_two - unit_two * jnp.mean(grad_unit_two * unit_two, axis=-1, keepdims=True)
    )
    hidden_low = grad_hidden.astype(jnp.bfloat16)
    grad_output_t = contract_rows(hidden_low, gated)
    grad_gated = project(hidden_low, output_t)
    grad_attended = (grad_gated * gate_open).astype(jnp.bfloat16)
    grad_gate_pre = (grad_gated * attended_flat * gate_open * (1.0 - gate_open)).astype(
        jnp.bfloat16
    )
    grad_query, grad_key, grad_value, grad_log = lax.map(
        attend_backward,
        (
            query_all,
            key_all,
            value_all,
            log_forget,
            piece_starts,
            attended,
            normalizer,
            head_view(grad_attended),
        ),
    )
    grad_forget = (grad_log.reshape(row_count, heads_here) * jax.nn.sigmoid(-forget_pre)).astype(
        jnp.bfloat16
    )
    grad_five = jnp.concatenate(
        [
            grad_query.reshape(row_count, share_width),
            grad_key.reshape(row_count, share_width),
            grad_value.reshape(row_count, share_width),
            grad_gate_pre,
            grad_forget,
        ],
        axis=1,
    )
    output = (hidden + ffn_out).astype(jnp.bfloat16).reshape(tokens.shape)
    grad_bias = jnp.sum(grad_forget.astype(jnp.float32), axis=0)
    place = jnp.arange(width, dtype=jnp.int32) % block
    bias_col = jnp.where(
        place < heads_here, jnp.take(grad_bias, jnp.minimum(place, heads_here - 1)), 0.0
    )
    late_grads = lax.dot_general(
        grad_five, normed, (((0,), (0,)), ((), ())), preferred_element_type=jnp.float32
    ).T
    grad_normed = tensor_sum(contract_cols(grad_five, joined_five).astype(jnp.bfloat16), "tensor")
    grad_attn_gain = jnp.sum(grad_normed * unit_one, axis=0)
    late_sums = ring_reduce_scatter(
        jnp.concatenate(
            [
                late_grads,
                bias_col[:, None],
                grad_attn_gain[:, None],
                grad_ffn_gain[:, None],
                grad_output_t,
            ],
            axis=1,
        ),
        "dp",
    )
    out_at = 4 * share_width + heads_here + 3
    grad_unit_one = grad_normed * gain_one
    grad_inputs = grad_hidden + scale_one * (
        grad_unit_one - unit_one * jnp.mean(grad_unit_one * unit_one, axis=-1, keepdims=True)
    )
    tokens_grad = grad_inputs.astype(jnp.bfloat16).reshape(tokens.shape)
    forget_at = 4 * share_width
    return (
        output,
        tokens_grad,
        late_sums[:, forget_at + heads_here + 1],
        late_sums[:, :share_width],
        late_sums[:, share_width : 2 * share_width],
        late_sums[:, 2 * share_width : 3 * share_width],
        late_sums[:, 3 * share_width : 4 * share_width],
        late_sums[:, forget_at : forget_at + heads_here],
        late_sums[:heads_here, forget_at + heads_here],
        late_sums[:, out_at : out_at + share_width].T,
        late_sums[:, out_at - 1],
        ffn_sums[:, :units],
        ffn_sums[:, units : 2 * units],
        ffn_sums[:, 2 * units : 3 * units].T,
    )


def solution(mesh):
    placed = (
        P("dp", None, None),
        P("dp", None),
        P("dp"),
        P("dp", "tensor"),
        P("dp", "tensor"),
        P("dp", "tensor"),
        P("dp", "tensor"),
        P("dp", "tensor"),
        P("tensor"),
        P("tensor", "dp"),
        P("dp"),
        P("dp", "tensor"),
        P("dp", "tensor"),
        P("tensor", "dp"),
        P("dp", None, None),
    )
    return jax.shard_map(
        on_device,
        mesh=mesh,
        in_specs=placed,
        out_specs=(
            P("dp", None, None),
            P("dp", None, None),
            P("dp"),
            P("dp", "tensor"),
            P("dp", "tensor"),
            P("dp", "tensor"),
            P("dp", "tensor"),
            P("dp", "tensor"),
            P("tensor"),
            P("tensor", "dp"),
            P("dp"),
            P("dp", "tensor"),
            P("dp", "tensor"),
            P("tensor", "dp"),
        ),
        check_vma=False,
    )
```

```python
import jax
import jax.numpy as jnp
from jax import lax
from jax.sharding import PartitionSpec as P

PIECE = 256


epsilon = 1e-06
masked_value = -1e30


def project(left, right):
    return jnp.dot(left, right, preferred_element_type=jnp.float32)


def contract_rows(left, right):
    return lax.dot_general(
        left, right, (((0,), (0,)), ((), ())), preferred_element_type=jnp.float32
    )


def contract_cols(left, right):
    return lax.dot_general(
        left, right, (((1,), (1,)), ((), ())), preferred_element_type=jnp.float32
    )


def allowed_pairs(starts, length):
    places = jnp.arange(length, dtype=jnp.int32)
    inside = (
        (starts[:, None] >= 0)
        & (places[None, :] >= starts[:, None])
        & (places[None, :] < starts[:, None] + PIECE)
    )
    labels = jnp.sum(
        jnp.where(inside, jnp.arange(1, starts.shape[0] + 1, dtype=jnp.int32)[:, None], 0), axis=0
    )
    same = (labels[:, None] == labels[None, :]) & (labels[:, None] > 0)
    return (places[None, :] <= places[:, None]) | same


def key_reach(first_row, block_rows, length, slots):
    width = length // slots
    return min(length, -(-(first_row + block_rows) // width) * width)


def block_scores(query_rows, key_all, decay, allowed_rows, first_row):
    count = query_rows.shape[0]
    reach = key_all.shape[0]
    raw = jnp.einsum(
        "qhd,khd->hqk", query_rows, key_all, preferred_element_type=jnp.float32
    ) * query_rows.shape[-1] ** (-0.5)
    apart = (
        lax.slice_in_dim(decay, first_row, first_row + count, axis=1)[:, :, None]
        - decay[:, None, :reach]
    )
    return (jnp.where(allowed_rows[None], raw - jnp.abs(apart), masked_value), apart)


def attend_forward(items):
    query_all, key_all, value_all, log_forget, starts = items
    length = query_all.shape[0]
    block_rows = min(512, length)
    decay = jnp.cumsum(log_forget, axis=0).T
    allowed = allowed_pairs(starts, length)
    results = []
    normalizers = []
    for first_row in range(0, length, block_rows):
        reach = key_reach(first_row, block_rows, length, starts.shape[0])
        scores, apart = block_scores(
            query_all[first_row : first_row + block_rows],
            key_all[:reach],
            decay,
            allowed[first_row : first_row + block_rows, :reach],
            first_row,
        )
        largest = jnp.max(scores, axis=-1, keepdims=True)
        weights = jnp.exp(scores - largest)
        denominator = jnp.sum(weights, axis=-1, keepdims=True)
        chances = (weights / denominator).astype(jnp.bfloat16)
        results.append(
            jnp.einsum(
                "hqk,khd->qhd", chances, value_all[:reach], preferred_element_type=jnp.float32
            )
        )
        normalizers.append(largest + jnp.log(denominator))
    return (jnp.concatenate(results, axis=0), jnp.concatenate(normalizers, axis=1))


def attend_backward(items):
    query_all, key_all, value_all, log_forget, starts, attended, normalizer, grad_out = items
    length = query_all.shape[0]
    block_rows = min(512, length)
    scale = query_all.shape[-1] ** (-0.5)
    decay = jnp.cumsum(log_forget, axis=0).T
    allowed = allowed_pairs(starts, length)
    grad_key = jnp.zeros(key_all.shape, jnp.float32)
    grad_value = jnp.zeros(value_all.shape, jnp.float32)
    grad_decay = jnp.zeros(decay.shape, jnp.float32)
    query_parts = []
    row_parts = []
    for first_row in range(0, length, block_rows):
        reach = key_reach(first_row, block_rows, length, starts.shape[0])
        key_rows = key_all[:reach]
        value_rows = value_all[:reach]
        query_rows = query_all[first_row : first_row + block_rows]
        out_rows = grad_out[first_row : first_row + block_rows]
        scores, apart = block_scores(
            query_rows, key_rows, decay, allowed[first_row : first_row + block_rows, :reach],
            first_row,
        )
        chances = jnp.exp(scores - normalizer[:, first_row : first_row + block_rows])
        grad_chance = jnp.einsum(
            "qhd,khd->hqk", out_rows, value_rows, preferred_element_type=jnp.float32
        )
        offset = jnp.sum(
            out_rows.astype(jnp.float32) * attended[first_row : first_row + block_rows], axis=-1
        ).T[:, :, None]
        grad_score = chances * (grad_chance - offset)
        grad_rounded = grad_score.astype(jnp.bfloat16)
        grad_value = grad_value.at[:reach].add(
            jnp.einsum(
                "hqk,qhd->khd",
                chances.astype(jnp.bfloat16),
                out_rows,
                preferred_element_type=jnp.float32,
            )
        )
        grad_key = grad_key.at[:reach].add(
            jnp.einsum(
                "hqk,qhd->khd", grad_rounded, query_rows, preferred_element_type=jnp.float32
            )
            * scale
        )
        query_parts.append(
            jnp.einsum("hqk,khd->qhd", grad_rounded, key_rows, preferred_element_type=jnp.float32)
            * scale
        )
        signed = grad_score * jnp.sign(apart)
        grad_decay = grad_decay.at[:, :reach].add(jnp.sum(signed, axis=1))
        row_parts.append(-jnp.sum(signed, axis=-1))
    grad_decay = grad_decay + jnp.concatenate(row_parts, axis=1)
    grad_log = jnp.flip(jnp.cumsum(jnp.flip(grad_decay, axis=1), axis=1), axis=1).T
    grad_query = jnp.concatenate(query_parts, axis=0)
    return (
        grad_query.astype(jnp.bfloat16),
        grad_key.astype(jnp.bfloat16),
        grad_value.astype(jnp.bfloat16),
        grad_log,
    )


def ring_order(n):
    inner = 2 if n % 2 == 0 else 1
    outer = n // inner
    order = [o * inner for o in range(outer)]
    if inner == 2:
        order += [o * inner + 1 for o in reversed(range(outer))]
    return order


def ring_tables(n):
    order = ring_order(n)
    where = [0] * n
    for p, d in enumerate(order):
        where[d] = p
    to_next = [(order[p], order[(p + 1) % n]) for p in range(n)]
    to_prev = [(order[p], order[(p - 1) % n]) for p in range(n)]
    return order, where, to_next, to_prev


def ring_gather(local, axis):
    n = lax.axis_size(axis)
    rows = local.shape[0]
    if n > 16:
        return lax.all_gather(local, axis, axis=0, tiled=True)
    order, where, to_next, to_prev = ring_tables(n)
    me = lax.axis_index(axis)
    out = jnp.zeros((n, rows) + local.shape[1:], local.dtype)
    out = lax.dynamic_update_index_in_dim(out, local, me, axis=0)
    ahead = n // 2
    behind = n - 1 - ahead
    moving_next = local
    moving_prev = local
    for step in range(1, ahead + 1):
        moving_next = lax.ppermute(moving_next, axis, to_next)
        source = jnp.asarray([order[(where[d] - step) % n] for d in range(n)], jnp.int32)[me]
        out = lax.dynamic_update_index_in_dim(out, moving_next, source, axis=0)
        if step <= behind:
            moving_prev = lax.ppermute(moving_prev, axis, to_prev)
            source = jnp.asarray([order[(where[d] + step) % n] for d in range(n)], jnp.int32)[me]
            out = lax.dynamic_update_index_in_dim(out, moving_prev, source, axis=0)
    return out.reshape((n * rows,) + local.shape[1:])


def ring_reduce_scatter(full, axis):
    n = lax.axis_size(axis)
    rows = full.shape[0] // n
    if n > 16:
        return lax.psum_scatter(
            full.astype(jnp.bfloat16), axis, scatter_dimension=0, tiled=True
        ).astype(jnp.float32)
    order, where, to_next, to_prev = ring_tables(n)
    me = lax.axis_index(axis)

    def chunk(shift):
        index = jnp.asarray([order[(where[d] + shift) % n] for d in range(n)], jnp.int32)[me]
        return lax.dynamic_slice_in_dim(full, index * rows, rows, axis=0)

    ahead = n // 2
    behind = n - 1 - ahead
    part_next = None
    part_prev = None
    for step in range(ahead):
        mine = chunk(ahead - step)
        part_next = mine if part_next is None else part_next.astype(jnp.float32) + mine
        part_next = lax.ppermute(part_next.astype(jnp.bfloat16), axis, to_next)
        if step < behind:
            mine = chunk(step - behind)
            part_prev = mine if part_prev is None else part_prev.astype(jnp.float32) + mine
            part_prev = lax.ppermute(part_prev.astype(jnp.bfloat16), axis, to_prev)
    total = lax.dynamic_slice_in_dim(full, me * rows, rows, axis=0) + part_next.astype(jnp.float32)
    if part_prev is not None:
        total = total + part_prev.astype(jnp.float32)
    return total


def tensor_sum(term, axis):
    n = lax.axis_size(axis)
    if n != 4:
        return lax.psum(term, axis).astype(jnp.float32)
    half = term.shape[0] // 2
    me = lax.axis_index(axis)
    core = me % 2
    keep = lax.dynamic_slice_in_dim(term, core * half, half, axis=0)
    give = lax.dynamic_slice_in_dim(term, (1 - core) * half, half, axis=0)
    on_chip = [(i, i ^ 1) for i in range(n)]
    across = [(i, i ^ 2) for i in range(n)]
    mine = keep.astype(jnp.float32) + lax.ppermute(give, axis, on_chip).astype(jnp.float32)
    total = mine + lax.ppermute(mine.astype(term.dtype), axis, across).astype(jnp.float32)
    back = lax.ppermute(total.astype(term.dtype), axis, on_chip).astype(jnp.float32)
    first = jnp.where(core == 0, total, back)
    second = jnp.where(core == 0, back, total)
    return jnp.concatenate([first, second], axis=0)


def on_device(
    tokens,
    piece_starts,
    attn_gain,
    w_query,
    w_key,
    w_value,
    w_outgate,
    w_forget,
    forget_bias,
    w_output,
    ffn_gain,
    w_gate,
    w_up,
    w_down,
    cotangent,
):
    sequences, length, width = tokens.shape
    heads_here = w_forget.shape[1]
    share_width = w_query.shape[1]
    head_size = share_width // heads_here
    row_count = sequences * length
    block = w_query.shape[0]
    units = w_gate.shape[1]

    def head_view(values):
        return values.reshape(sequences, length, heads_here, head_size)

    attn_local = jnp.concatenate(
        [w_output.T, w_query, w_key, w_value, w_outgate, w_forget, attn_gain[:, None]], axis=1
    )
    attn_full = ring_gather(attn_local, "dp")
    ffn_local = jnp.concatenate([w_gate, w_up, w_down.T, ffn_gain[:, None]], axis=1)
    ffn_local, attn_full = lax.optimization_barrier((ffn_local, attn_full))
    output_t = attn_full[:, :share_width]
    joined = attn_full[:, share_width : 5 * share_width]
    joined_five = attn_full[:, share_width : 5 * share_width + heads_here]
    forget_w = attn_full[:, 5 * share_width : 5 * share_width + heads_here]
    gain_one = attn_full[:, 5 * share_width + heads_here].astype(jnp.float32)
    ffn_full = lax.all_gather(ffn_local, "dp", axis=0, tiled=True)
    gate_up_w = ffn_full[:, : 2 * units]
    down_t = ffn_full[:, 2 * units : 3 * units]
    gain_two = ffn_full[:, 3 * units].astype(jnp.float32)

    inputs = tokens.reshape(row_count, width).astype(jnp.float32)
    scale_one = lax.rsqrt(jnp.mean(inputs * inputs, axis=-1, keepdims=True) + epsilon)
    unit_one = inputs * scale_one
    normed = (unit_one * gain_one).astype(jnp.bfloat16)
    projected = project(normed, joined)
    query_all = head_view(projected[:, :share_width].astype(jnp.bfloat16))
    key_all = head_view(projected[:, share_width : 2 * share_width].astype(jnp.bfloat16))
    value_all = head_view(projected[:, 2 * share_width : 3 * share_width].astype(jnp.bfloat16))
    gate_pre = projected[:, 3 * share_width :]
    forget_pre = project(normed, forget_w) + forget_bias[None, :]
    log_forget = jax.nn.log_sigmoid(forget_pre).reshape(sequences, length, heads_here)
    attended, normalizer = lax.map(
        attend_forward, (query_all, key_all, value_all, log_forget, piece_starts)
    )
    attended_flat = attended.reshape(row_count, share_width)
    gate_open = jax.nn.sigmoid(gate_pre)
    gated = (attended_flat * gate_open).astype(jnp.bfloat16)
    attention = tensor_sum(contract_cols(gated, output_t).astype(jnp.bfloat16), "tensor")
    hidden = inputs + attention
    scale_two = lax.rsqrt(jnp.mean(hidden * hidden, axis=-1, keepdims=True) + epsilon)
    unit_two = hidden * scale_two
    normed_two = (unit_two * gain_two).astype(jnp.bfloat16)
    inner_pre = project(normed_two, gate_up_w)
    gate_part = inner_pre[:, :units]
    up_part = inner_pre[:, units:]
    inner = (jax.nn.silu(gate_part) * up_part).astype(jnp.bfloat16)
    ffn_term = contract_cols(inner, down_t).astype(jnp.bfloat16)
    upstream_low = cotangent.reshape(row_count, width)
    upstream = upstream_low.astype(jnp.float32)
    grad_inner = project(upstream_low, down_t)
    sigma = jax.nn.sigmoid(gate_part)
    grad_gate = (grad_inner * up_part * sigma * (1.0 + gate_part * (1.0 - sigma))).astype(
        jnp.bfloat16
    )
    grad_up = (grad_inner * gate_part * sigma).astype(jnp.bfloat16)
    grad_gate_up = jnp.concatenate([grad_gate, grad_up], axis=1)
    grad_down_t = contract_rows(upstream_low, inner)
    grad_gate_up_w = contract_rows(normed_two, grad_gate_up)
    ffn_grads = jnp.concatenate([grad_gate_up_w, grad_down_t], axis=1).astype(jnp.bfloat16)
    grad_normed_two = tensor_sum(
        contract_cols(grad_gate_up, gate_up_w).astype(jnp.bfloat16), "tensor"
    )
    ffn_grads, grad_normed_two = lax.optimization_barrier((ffn_grads, grad_normed_two))
    ffn_sums = lax.psum_scatter(ffn_grads, "dp", scatter_dimension=0, tiled=True).astype(
        jnp.float32
    )
    ffn_term, grad_normed_two = lax.optimization_barrier((ffn_term, grad_normed_two))
    ffn_out = tensor_sum(ffn_term, "tensor")
    grad_ffn_gain = jnp.sum(grad_normed_two * unit_two, axis=0)
    grad_unit_two = grad_normed_two * gain_two
    grad_hidden = upstream + scale_two * (
        grad_unit_two - unit_two * jnp.mean(grad_unit_two * unit_two, axis=-1, keepdims=True)
    )
    hidden_low = grad_hidden.astype(jnp.bfloat16)
    grad_output_t = contract_rows(hidden_low, gated)
    grad_gated = project(hidden_low, output_t)
    grad_attended = (grad_gated * gate_open).astype(jnp.bfloat16)
    grad_gate_pre = (grad_gated * attended_flat * gate_open * (1.0 - gate_open)).astype(
        jnp.bfloat16
    )
    grad_query, grad_key, grad_value, grad_log = lax.map(
        attend_backward,
        (
            query_all,
            key_all,
            value_all,
            log_forget,
            piece_starts,
            attended,
            normalizer,
            head_view(grad_attended),
        ),
    )
    grad_forget = (grad_log.reshape(row_count, heads_here) * jax.nn.sigmoid(-forget_pre)).astype(
        jnp.bfloat16
    )
    grad_five = jnp.concatenate(
        [
            grad_query.reshape(row_count, share_width),
            grad_key.reshape(row_count, share_width),
            grad_value.reshape(row_count, share_width),
            grad_gate_pre,
            grad_forget,
        ],
        axis=1,
    )
    output = (hidden + ffn_out).astype(jnp.bfloat16).reshape(tokens.shape)
    grad_bias = jnp.sum(grad_forget.astype(jnp.float32), axis=0)
    place = jnp.arange(width, dtype=jnp.int32) % block
    bias_col = jnp.where(
        place < heads_here, jnp.take(grad_bias, jnp.minimum(place, heads_here - 1)), 0.0
    )
    late_grads = lax.dot_general(
        grad_five, normed, (((0,), (0,)), ((), ())), preferred_element_type=jnp.float32
    ).T
    grad_normed = tensor_sum(contract_cols(grad_five, joined_five).astype(jnp.bfloat16), "tensor")
    grad_attn_gain = jnp.sum(grad_normed * unit_one, axis=0)
    late_sums = ring_reduce_scatter(
        jnp.concatenate(
            [
                late_grads,
                bias_col[:, None],
                grad_attn_gain[:, None],
                grad_ffn_gain[:, None],
                grad_output_t,
            ],
            axis=1,
        ),
        "dp",
    )
    out_at = 4 * share_width + heads_here + 3
    grad_unit_one = grad_normed * gain_one
    grad_inputs = grad_hidden + scale_one * (
        grad_unit_one - unit_one * jnp.mean(grad_unit_one * unit_one, axis=-1, keepdims=True)
    )
    tokens_grad = grad_inputs.astype(jnp.bfloat16).reshape(tokens.shape)
    forget_at = 4 * share_width
    return (
        output,
        tokens_grad,
        late_sums[:, forget_at + heads_here + 1],
        late_sums[:, :share_width],
        late_sums[:, share_width : 2 * share_width],
        late_sums[:, 2 * share_width : 3 * share_width],
        late_sums[:, 3 * share_width : 4 * share_width],
        late_sums[:, forget_at : forget_at + heads_here],
        late_sums[:heads_here, forget_at + heads_here],
        late_sums[:, out_at : out_at + share_width].T,
        late_sums[:, out_at - 1],
        ffn_sums[:, :units],
        ffn_sums[:, units : 2 * units],
        ffn_sums[:, 2 * units : 3 * units].T,
    )


def solution(mesh):
    placed = (
        P("dp", None, None),
        P("dp", None),
        P("dp"),
        P("dp", "tensor"),
        P("dp", "tensor"),
        P("dp", "tensor"),
        P("dp", "tensor"),
        P("dp", "tensor"),
        P("tensor"),
        P("tensor", "dp"),
        P("dp"),
        P("dp", "tensor"),
        P("dp", "tensor"),
        P("tensor", "dp"),
        P("dp", None, None),
    )
    return jax.shard_map(
        on_device,
        mesh=mesh,
        in_specs=placed,
        out_specs=(
            P("dp", None, None),
            P("dp", None, None),
            P("dp"),
            P("dp", "tensor"),
            P("dp", "tensor"),
            P("dp", "tensor"),
            P("dp", "tensor"),
            P("dp", "tensor"),
            P("tensor"),
            P("tensor", "dp"),
            P("dp"),
            P("dp", "tensor"),
            P("dp", "tensor"),
            P("tensor", "dp"),
        ),
        check_vma=False,
    )
```

```python
import jax
import jax.numpy as jnp
from jax import lax
from jax.sharding import PartitionSpec as P

PIECE = 256


epsilon = 1e-06
masked_value = -1e30


def project(left, right):
    return jnp.dot(left, right, preferred_element_type=jnp.float32)


def contract_rows(left, right):
    return lax.dot_general(
        left, right, (((0,), (0,)), ((), ())), preferred_element_type=jnp.float32
    )


def contract_cols(left, right):
    return lax.dot_general(
        left, right, (((1,), (1,)), ((), ())), preferred_element_type=jnp.float32
    )


def allowed_pairs(starts, length):
    places = jnp.arange(length, dtype=jnp.int32)
    inside = (
        (starts[:, None] >= 0)
        & (places[None, :] >= starts[:, None])
        & (places[None, :] < starts[:, None] + PIECE)
    )
    labels = jnp.sum(
        jnp.where(inside, jnp.arange(1, starts.shape[0] + 1, dtype=jnp.int32)[:, None], 0), axis=0
    )
    same = (labels[:, None] == labels[None, :]) & (labels[:, None] > 0)
    return (places[None, :] <= places[:, None]) | same


def key_reach(first_row, block_rows, length, slots):
    width = length // slots
    return min(length, -(-(first_row + block_rows) // width) * width)


def block_scores(query_rows, key_all, decay, allowed_rows, first_row):
    count = query_rows.shape[0]
    reach = key_all.shape[0]
    raw = jnp.einsum(
        "qhd,khd->hqk", query_rows, key_all, preferred_element_type=jnp.float32
    ) * query_rows.shape[-1] ** (-0.5)
    apart = (
        lax.slice_in_dim(decay, first_row, first_row + count, axis=1)[:, :, None]
        - decay[:, None, :reach]
    )
    return (jnp.where(allowed_rows[None], raw - jnp.abs(apart), masked_value), apart)


def running_sum(values, reverse=False):
    length = values.shape[1]
    earlier = lax.broadcasted_iota(jnp.int32, (length, length), 0)
    later = lax.broadcasted_iota(jnp.int32, (length, length), 1)
    keep = earlier >= later if reverse else earlier <= later
    return jnp.dot(
        values,
        keep.astype(jnp.float32),
        precision=lax.Precision.HIGHEST,
        preferred_element_type=jnp.float32,
    )


def attend_forward(items):
    query_all, key_all, value_all, log_forget, starts = items
    length = query_all.shape[0]
    block_rows = min(512, length)
    decay = running_sum(log_forget.T)
    allowed = allowed_pairs(starts, length)
    results = []
    normalizers = []
    for first_row in range(0, length, block_rows):
        reach = key_reach(first_row, block_rows, length, starts.shape[0])
        scores, apart = block_scores(
            query_all[first_row : first_row + block_rows],
            key_all[:reach],
            decay,
            allowed[first_row : first_row + block_rows, :reach],
            first_row,
        )
        largest = jnp.max(scores, axis=-1, keepdims=True)
        weights = jnp.exp(scores - largest)
        denominator = jnp.sum(weights, axis=-1, keepdims=True)
        chances = (weights / denominator).astype(jnp.bfloat16)
        results.append(
            jnp.einsum(
                "hqk,khd->qhd", chances, value_all[:reach], preferred_element_type=jnp.float32
            )
        )
        normalizers.append(largest + jnp.log(denominator))
    return (jnp.concatenate(results, axis=0), jnp.concatenate(normalizers, axis=1))


def attend_backward(items):
    query_all, key_all, value_all, log_forget, starts, attended, normalizer, grad_out = items
    length = query_all.shape[0]
    block_rows = min(512, length)
    scale = query_all.shape[-1] ** (-0.5)
    decay = running_sum(log_forget.T)
    allowed = allowed_pairs(starts, length)
    grad_key = jnp.zeros(key_all.shape, jnp.float32)
    grad_value = jnp.zeros(value_all.shape, jnp.float32)
    grad_decay = jnp.zeros(decay.shape, jnp.float32)
    query_parts = []
    row_parts = []
    for first_row in range(0, length, block_rows):
        reach = key_reach(first_row, block_rows, length, starts.shape[0])
        key_rows = key_all[:reach]
        value_rows = value_all[:reach]
        query_rows = query_all[first_row : first_row + block_rows]
        out_rows = grad_out[first_row : first_row + block_rows]
        scores, apart = block_scores(
            query_rows, key_rows, decay, allowed[first_row : first_row + block_rows, :reach],
            first_row,
        )
        chances = jnp.exp(scores - normalizer[:, first_row : first_row + block_rows])
        grad_chance = jnp.einsum(
            "qhd,khd->hqk", out_rows, value_rows, preferred_element_type=jnp.float32
        )
        offset = jnp.sum(
            out_rows.astype(jnp.float32) * attended[first_row : first_row + block_rows], axis=-1
        ).T[:, :, None]
        grad_score = chances * (grad_chance - offset)
        grad_rounded = grad_score.astype(jnp.bfloat16)
        grad_value = grad_value.at[:reach].add(
            jnp.einsum(
                "hqk,qhd->khd",
                chances.astype(jnp.bfloat16),
                out_rows,
                preferred_element_type=jnp.float32,
            )
        )
        grad_key = grad_key.at[:reach].add(
            jnp.einsum(
                "hqk,qhd->khd", grad_rounded, query_rows, preferred_element_type=jnp.float32
            )
            * scale
        )
        query_parts.append(
            jnp.einsum("hqk,khd->qhd", grad_rounded, key_rows, preferred_element_type=jnp.float32)
            * scale
        )
        signed = grad_score * jnp.sign(apart)
        grad_decay = grad_decay.at[:, :reach].add(jnp.sum(signed, axis=1))
        row_parts.append(-jnp.sum(signed, axis=-1))
    grad_decay = grad_decay + jnp.concatenate(row_parts, axis=1)
    grad_log = running_sum(grad_decay, reverse=True).T
    grad_query = jnp.concatenate(query_parts, axis=0)
    return (
        grad_query.astype(jnp.bfloat16),
        grad_key.astype(jnp.bfloat16),
        grad_value.astype(jnp.bfloat16),
        grad_log,
    )


def ring_order(n):
    inner = 2 if n % 2 == 0 else 1
    outer = n // inner
    order = [o * inner for o in range(outer)]
    if inner == 2:
        order += [o * inner + 1 for o in reversed(range(outer))]
    return order


def ring_tables(n):
    order = ring_order(n)
    where = [0] * n
    for p, d in enumerate(order):
        where[d] = p
    to_next = [(order[p], order[(p + 1) % n]) for p in range(n)]
    to_prev = [(order[p], order[(p - 1) % n]) for p in range(n)]
    return order, where, to_next, to_prev


def ring_gather(local, axis):
    n = lax.axis_size(axis)
    rows = local.shape[0]
    if n > 16:
        return lax.all_gather(local, axis, axis=0, tiled=True)
    order, where, to_next, to_prev = ring_tables(n)
    me = lax.axis_index(axis)
    out = jnp.zeros((n, rows) + local.shape[1:], local.dtype)
    out = lax.dynamic_update_index_in_dim(out, local, me, axis=0)
    ahead = n // 2
    behind = n - 1 - ahead
    moving_next = local
    moving_prev = local
    for step in range(1, ahead + 1):
        moving_next = lax.ppermute(moving_next, axis, to_next)
        source = jnp.asarray([order[(where[d] - step) % n] for d in range(n)], jnp.int32)[me]
        out = lax.dynamic_update_index_in_dim(out, moving_next, source, axis=0)
        if step <= behind:
            moving_prev = lax.ppermute(moving_prev, axis, to_prev)
            source = jnp.asarray([order[(where[d] + step) % n] for d in range(n)], jnp.int32)[me]
            out = lax.dynamic_update_index_in_dim(out, moving_prev, source, axis=0)
    return out.reshape((n * rows,) + local.shape[1:])


def ring_reduce_scatter(full, axis):
    n = lax.axis_size(axis)
    rows = full.shape[0] // n
    if n > 16:
        return lax.psum_scatter(
            full.astype(jnp.bfloat16), axis, scatter_dimension=0, tiled=True
        ).astype(jnp.float32)
    order, where, to_next, to_prev = ring_tables(n)
    me = lax.axis_index(axis)

    def chunk(shift):
        index = jnp.asarray([order[(where[d] + shift) % n] for d in range(n)], jnp.int32)[me]
        return lax.dynamic_slice_in_dim(full, index * rows, rows, axis=0)

    ahead = n // 2
    behind = n - 1 - ahead
    part_next = None
    part_prev = None
    for step in range(ahead):
        mine = chunk(ahead - step)
        part_next = mine if part_next is None else part_next.astype(jnp.float32) + mine
        part_next = lax.ppermute(part_next.astype(jnp.bfloat16), axis, to_next)
        if step < behind:
            mine = chunk(step - behind)
            part_prev = mine if part_prev is None else part_prev.astype(jnp.float32) + mine
            part_prev = lax.ppermute(part_prev.astype(jnp.bfloat16), axis, to_prev)
    total = lax.dynamic_slice_in_dim(full, me * rows, rows, axis=0) + part_next.astype(jnp.float32)
    if part_prev is not None:
        total = total + part_prev.astype(jnp.float32)
    return total


def tensor_sum(term, axis):
    n = lax.axis_size(axis)
    if n != 4:
        return lax.psum(term, axis).astype(jnp.float32)
    half = term.shape[0] // 2
    me = lax.axis_index(axis)
    core = me % 2
    keep = lax.dynamic_slice_in_dim(term, core * half, half, axis=0)
    give = lax.dynamic_slice_in_dim(term, (1 - core) * half, half, axis=0)
    on_chip = [(i, i ^ 1) for i in range(n)]
    across = [(i, i ^ 2) for i in range(n)]
    mine = keep.astype(jnp.float32) + lax.ppermute(give, axis, on_chip).astype(jnp.float32)
    total = mine + lax.ppermute(mine.astype(term.dtype), axis, across).astype(jnp.float32)
    back = lax.ppermute(total.astype(term.dtype), axis, on_chip).astype(jnp.float32)
    first = jnp.where(core == 0, total, back)
    second = jnp.where(core == 0, back, total)
    return jnp.concatenate([first, second], axis=0)


def on_device(
    tokens,
    piece_starts,
    attn_gain,
    w_query,
    w_key,
    w_value,
    w_outgate,
    w_forget,
    forget_bias,
    w_output,
    ffn_gain,
    w_gate,
    w_up,
    w_down,
    cotangent,
):
    sequences, length, width = tokens.shape
    heads_here = w_forget.shape[1]
    share_width = w_query.shape[1]
    head_size = share_width // heads_here
    row_count = sequences * length
    block = w_query.shape[0]
    units = w_gate.shape[1]

    def head_view(values):
        return values.reshape(sequences, length, heads_here, head_size)

    attn_local = jnp.concatenate(
        [w_output.T, w_query, w_key, w_value, w_outgate, w_forget, attn_gain[:, None]], axis=1
    )
    attn_full = ring_gather(attn_local, "dp")
    ffn_local = jnp.concatenate([w_gate, w_up, w_down.T, ffn_gain[:, None]], axis=1)
    ffn_local, attn_full = lax.optimization_barrier((ffn_local, attn_full))
    output_t = attn_full[:, :share_width]
    joined = attn_full[:, share_width : 5 * share_width]
    joined_five = attn_full[:, share_width : 5 * share_width + heads_here]
    forget_w = attn_full[:, 5 * share_width : 5 * share_width + heads_here]
    gain_one = attn_full[:, 5 * share_width + heads_here].astype(jnp.float32)
    ffn_full = lax.all_gather(ffn_local, "dp", axis=0, tiled=True)
    gate_up_w = ffn_full[:, : 2 * units]
    down_t = ffn_full[:, 2 * units : 3 * units]
    gain_two = ffn_full[:, 3 * units].astype(jnp.float32)

    inputs = tokens.reshape(row_count, width).astype(jnp.float32)
    scale_one = lax.rsqrt(jnp.mean(inputs * inputs, axis=-1, keepdims=True) + epsilon)
    unit_one = inputs * scale_one
    normed = (unit_one * gain_one).astype(jnp.bfloat16)
    projected = project(normed, joined)
    query_all = head_view(projected[:, :share_width].astype(jnp.bfloat16))
    key_all = head_view(projected[:, share_width : 2 * share_width].astype(jnp.bfloat16))
    value_all = head_view(projected[:, 2 * share_width : 3 * share_width].astype(jnp.bfloat16))
    gate_pre = projected[:, 3 * share_width :]
    forget_pre = project(normed, forget_w) + forget_bias[None, :]
    log_forget = jax.nn.log_sigmoid(forget_pre).reshape(sequences, length, heads_here)
    attended, normalizer = lax.map(
        attend_forward, (query_all, key_all, value_all, log_forget, piece_starts)
    )
    attended_flat = attended.reshape(row_count, share_width)
    gate_open = jax.nn.sigmoid(gate_pre)
    gated = (attended_flat * gate_open).astype(jnp.bfloat16)
    attention = tensor_sum(contract_cols(gated, output_t).astype(jnp.bfloat16), "tensor")
    hidden = inputs + attention
    scale_two = lax.rsqrt(jnp.mean(hidden * hidden, axis=-1, keepdims=True) + epsilon)
    unit_two = hidden * scale_two
    normed_two = (unit_two * gain_two).astype(jnp.bfloat16)
    inner_pre = project(normed_two, gate_up_w)
    gate_part = inner_pre[:, :units]
    up_part = inner_pre[:, units:]
    inner = (jax.nn.silu(gate_part) * up_part).astype(jnp.bfloat16)
    ffn_term = contract_cols(inner, down_t).astype(jnp.bfloat16)
    upstream_low = cotangent.reshape(row_count, width)
    upstream = upstream_low.astype(jnp.float32)
    grad_inner = project(upstream_low, down_t)
    sigma = jax.nn.sigmoid(gate_part)
    grad_gate = (grad_inner * up_part * sigma * (1.0 + gate_part * (1.0 - sigma))).astype(
        jnp.bfloat16
    )
    grad_up = (grad_inner * gate_part * sigma).astype(jnp.bfloat16)
    grad_gate_up = jnp.concatenate([grad_gate, grad_up], axis=1)
    grad_down_t = contract_rows(upstream_low, inner)
    grad_gate_up_w = contract_rows(normed_two, grad_gate_up)
    ffn_grads = jnp.concatenate([grad_gate_up_w, grad_down_t], axis=1).astype(jnp.bfloat16)
    grad_normed_two = tensor_sum(
        contract_cols(grad_gate_up, gate_up_w).astype(jnp.bfloat16), "tensor"
    )
    ffn_grads, grad_normed_two = lax.optimization_barrier((ffn_grads, grad_normed_two))
    ffn_sums = lax.psum_scatter(ffn_grads, "dp", scatter_dimension=0, tiled=True).astype(
        jnp.float32
    )
    ffn_term, grad_normed_two = lax.optimization_barrier((ffn_term, grad_normed_two))
    ffn_out = tensor_sum(ffn_term, "tensor")
    grad_ffn_gain = jnp.sum(grad_normed_two * unit_two, axis=0)
    grad_unit_two = grad_normed_two * gain_two
    grad_hidden = upstream + scale_two * (
        grad_unit_two - unit_two * jnp.mean(grad_unit_two * unit_two, axis=-1, keepdims=True)
    )
    hidden_low = grad_hidden.astype(jnp.bfloat16)
    grad_output_t = contract_rows(hidden_low, gated)
    grad_gated = project(hidden_low, output_t)
    grad_attended = (grad_gated * gate_open).astype(jnp.bfloat16)
    grad_gate_pre = (grad_gated * attended_flat * gate_open * (1.0 - gate_open)).astype(
        jnp.bfloat16
    )
    grad_query, grad_key, grad_value, grad_log = lax.map(
        attend_backward,
        (
            query_all,
            key_all,
            value_all,
            log_forget,
            piece_starts,
            attended,
            normalizer,
            head_view(grad_attended),
        ),
    )
    grad_forget = (grad_log.reshape(row_count, heads_here) * jax.nn.sigmoid(-forget_pre)).astype(
        jnp.bfloat16
    )
    grad_five = jnp.concatenate(
        [
            grad_query.reshape(row_count, share_width),
            grad_key.reshape(row_count, share_width),
            grad_value.reshape(row_count, share_width),
            grad_gate_pre,
            grad_forget,
        ],
        axis=1,
    )
    output = (hidden + ffn_out).astype(jnp.bfloat16).reshape(tokens.shape)
    grad_bias = jnp.sum(grad_forget.astype(jnp.float32), axis=0)
    place = jnp.arange(width, dtype=jnp.int32) % block
    bias_col = jnp.where(
        place < heads_here, jnp.take(grad_bias, jnp.minimum(place, heads_here - 1)), 0.0
    )
    late_grads = lax.dot_general(
        grad_five, normed, (((0,), (0,)), ((), ())), preferred_element_type=jnp.float32
    ).T
    grad_normed = tensor_sum(contract_cols(grad_five, joined_five).astype(jnp.bfloat16), "tensor")
    grad_attn_gain = jnp.sum(grad_normed * unit_one, axis=0)
    late_sums = ring_reduce_scatter(
        jnp.concatenate(
            [
                late_grads.astype(jnp.bfloat16),
                bias_col[:, None].astype(jnp.bfloat16),
                grad_attn_gain[:, None].astype(jnp.bfloat16),
                grad_ffn_gain[:, None].astype(jnp.bfloat16),
                grad_output_t.astype(jnp.bfloat16),
            ],
            axis=1,
        ),
        "dp",
    )
    out_at = 4 * share_width + heads_here + 3
    grad_unit_one = grad_normed * gain_one
    grad_inputs = grad_hidden + scale_one * (
        grad_unit_one - unit_one * jnp.mean(grad_unit_one * unit_one, axis=-1, keepdims=True)
    )
    tokens_grad = grad_inputs.astype(jnp.bfloat16).reshape(tokens.shape)
    forget_at = 4 * share_width
    return (
        output,
        tokens_grad,
        late_sums[:, forget_at + heads_here + 1],
        late_sums[:, :share_width],
        late_sums[:, share_width : 2 * share_width],
        late_sums[:, 2 * share_width : 3 * share_width],
        late_sums[:, 3 * share_width : 4 * share_width],
        late_sums[:, forget_at : forget_at + heads_here],
        late_sums[:heads_here, forget_at + heads_here],
        late_sums[:, out_at : out_at + share_width].T,
        late_sums[:, out_at - 1],
        ffn_sums[:, :units],
        ffn_sums[:, units : 2 * units],
        ffn_sums[:, 2 * units : 3 * units].T,
    )


def solution(mesh):
    placed = (
        P("dp", None, None),
        P("dp", None),
        P("dp"),
        P("dp", "tensor"),
        P("dp", "tensor"),
        P("dp", "tensor"),
        P("dp", "tensor"),
        P("dp", "tensor"),
        P("tensor"),
        P("tensor", "dp"),
        P("dp"),
        P("dp", "tensor"),
        P("dp", "tensor"),
        P("tensor", "dp"),
        P("dp", None, None),
    )
    return jax.shard_map(
        on_device,
        mesh=mesh,
        in_specs=placed,
        out_specs=(
            P("dp", None, None),
            P("dp", None, None),
            P("dp"),
            P("dp", "tensor"),
            P("dp", "tensor"),
            P("dp", "tensor"),
            P("dp", "tensor"),
            P("dp", "tensor"),
            P("tensor"),
            P("tensor", "dp"),
            P("dp"),
            P("dp", "tensor"),
            P("dp", "tensor"),
            P("tensor", "dp"),
        ),
        check_vma=False,
    )
```

```python
import jax
import jax.numpy as jnp
from jax import lax
from jax.sharding import PartitionSpec as P

PIECE = 256


epsilon = 1e-06
masked_value = -1e30


def project(left, right):
    return jnp.dot(left, right, preferred_element_type=jnp.float32)


def contract_rows(left, right):
    return lax.dot_general(
        left, right, (((0,), (0,)), ((), ())), preferred_element_type=jnp.float32
    )


def contract_cols(left, right):
    return lax.dot_general(
        left, right, (((1,), (1,)), ((), ())), preferred_element_type=jnp.float32
    )


def allowed_pairs(starts, length):
    places = jnp.arange(length, dtype=jnp.int32)
    inside = (
        (starts[:, None] >= 0)
        & (places[None, :] >= starts[:, None])
        & (places[None, :] < starts[:, None] + PIECE)
    )
    labels = jnp.sum(
        jnp.where(inside, jnp.arange(1, starts.shape[0] + 1, dtype=jnp.int32)[:, None], 0), axis=0
    )
    same = (labels[:, None] == labels[None, :]) & (labels[:, None] > 0)
    return (places[None, :] <= places[:, None]) | same


def key_reach(first_row, block_rows, length, slots):
    width = length // slots
    return min(length, -(-(first_row + block_rows) // width) * width)


def block_scores(query_rows, key_all, decay, allowed_rows, first_row):
    count = query_rows.shape[0]
    reach = key_all.shape[0]
    raw = jnp.einsum(
        "qhd,khd->hqk", query_rows, key_all, preferred_element_type=jnp.float32
    ) * query_rows.shape[-1] ** (-0.5)
    apart = (
        lax.slice_in_dim(decay, first_row, first_row + count, axis=1)[:, :, None]
        - decay[:, None, :reach]
    )
    return (jnp.where(allowed_rows[None], raw - jnp.abs(apart), masked_value), apart)


def running_sum(values, reverse=False):
    length = values.shape[1]
    earlier = lax.broadcasted_iota(jnp.int32, (length, length), 0)
    later = lax.broadcasted_iota(jnp.int32, (length, length), 1)
    keep = earlier >= later if reverse else earlier <= later
    return jnp.dot(
        values,
        keep.astype(jnp.float32),
        precision=lax.Precision.HIGHEST,
        preferred_element_type=jnp.float32,
    )


def attend_forward(items):
    query_all, key_all, value_all, log_forget, starts = items
    length = query_all.shape[0]
    block_rows = min(512, length)
    decay = running_sum(log_forget.T)
    allowed = allowed_pairs(starts, length)
    results = []
    normalizers = []
    for first_row in range(0, length, block_rows):
        reach = key_reach(first_row, block_rows, length, starts.shape[0])
        scores, apart = block_scores(
            query_all[first_row : first_row + block_rows],
            key_all[:reach],
            decay,
            allowed[first_row : first_row + block_rows, :reach],
            first_row,
        )
        largest = jnp.max(scores, axis=-1, keepdims=True)
        weights = jnp.exp(scores - largest)
        denominator = jnp.sum(weights, axis=-1, keepdims=True)
        chances = (weights / denominator).astype(jnp.bfloat16)
        results.append(
            jnp.einsum(
                "hqk,khd->qhd", chances, value_all[:reach], preferred_element_type=jnp.float32
            )
        )
        normalizers.append(largest + jnp.log(denominator))
    return (jnp.concatenate(results, axis=0), jnp.concatenate(normalizers, axis=1))


def attend_backward(items):
    query_all, key_all, value_all, log_forget, starts, attended, normalizer, grad_out = items
    length = query_all.shape[0]
    block_rows = min(512, length)
    scale = query_all.shape[-1] ** (-0.5)
    decay = running_sum(log_forget.T)
    allowed = allowed_pairs(starts, length)
    grad_key = jnp.zeros(key_all.shape, jnp.float32)
    grad_value = jnp.zeros(value_all.shape, jnp.float32)
    grad_decay = jnp.zeros(decay.shape, jnp.float32)
    query_parts = []
    row_parts = []
    for first_row in range(0, length, block_rows):
        reach = key_reach(first_row, block_rows, length, starts.shape[0])
        key_rows = key_all[:reach]
        value_rows = value_all[:reach]
        query_rows = query_all[first_row : first_row + block_rows]
        out_rows = grad_out[first_row : first_row + block_rows]
        scores, apart = block_scores(
            query_rows, key_rows, decay, allowed[first_row : first_row + block_rows, :reach],
            first_row,
        )
        chances = jnp.exp(scores - normalizer[:, first_row : first_row + block_rows])
        grad_chance = jnp.einsum(
            "qhd,khd->hqk", out_rows, value_rows, preferred_element_type=jnp.float32
        )
        offset = jnp.sum(
            out_rows.astype(jnp.float32) * attended[first_row : first_row + block_rows], axis=-1
        ).T[:, :, None]
        grad_score = chances * (grad_chance - offset)
        grad_rounded = grad_score.astype(jnp.bfloat16)
        grad_value = grad_value.at[:reach].add(
            jnp.einsum(
                "hqk,qhd->khd",
                chances.astype(jnp.bfloat16),
                out_rows,
                preferred_element_type=jnp.float32,
            )
        )
        grad_key = grad_key.at[:reach].add(
            jnp.einsum(
                "hqk,qhd->khd", grad_rounded, query_rows, preferred_element_type=jnp.float32
            )
            * scale
        )
        query_parts.append(
            jnp.einsum("hqk,khd->qhd", grad_rounded, key_rows, preferred_element_type=jnp.float32)
            * scale
        )
        signed = grad_score * jnp.sign(apart)
        grad_decay = grad_decay.at[:, :reach].add(jnp.sum(signed, axis=1))
        row_parts.append(-jnp.sum(signed, axis=-1))
    grad_decay = grad_decay + jnp.concatenate(row_parts, axis=1)
    grad_log = running_sum(grad_decay, reverse=True).T
    grad_query = jnp.concatenate(query_parts, axis=0)
    return (
        grad_query.astype(jnp.bfloat16),
        grad_key.astype(jnp.bfloat16),
        grad_value.astype(jnp.bfloat16),
        grad_log,
    )


def ring_order(n):
    inner = 2 if n % 2 == 0 else 1
    outer = n // inner
    order = [o * inner for o in range(outer)]
    if inner == 2:
        order += [o * inner + 1 for o in reversed(range(outer))]
    return order


def ring_tables(n):
    order = ring_order(n)
    where = [0] * n
    for p, d in enumerate(order):
        where[d] = p
    to_next = [(order[p], order[(p + 1) % n]) for p in range(n)]
    to_prev = [(order[p], order[(p - 1) % n]) for p in range(n)]
    return order, where, to_next, to_prev


def ring_gather(local, axis):
    n = lax.axis_size(axis)
    rows = local.shape[0]
    if n > 16:
        return lax.all_gather(local, axis, axis=0, tiled=True)
    order, where, to_next, to_prev = ring_tables(n)
    me = lax.axis_index(axis)
    out = jnp.zeros((n, rows) + local.shape[1:], local.dtype)
    out = lax.dynamic_update_index_in_dim(out, local, me, axis=0)
    ahead = n // 2
    behind = n - 1 - ahead
    moving_next = local
    moving_prev = local
    for step in range(1, ahead + 1):
        moving_next = lax.ppermute(moving_next, axis, to_next)
        source = jnp.asarray([order[(where[d] - step) % n] for d in range(n)], jnp.int32)[me]
        out = lax.dynamic_update_index_in_dim(out, moving_next, source, axis=0)
        if step <= behind:
            moving_prev = lax.ppermute(moving_prev, axis, to_prev)
            source = jnp.asarray([order[(where[d] + step) % n] for d in range(n)], jnp.int32)[me]
            out = lax.dynamic_update_index_in_dim(out, moving_prev, source, axis=0)
    return out.reshape((n * rows,) + local.shape[1:])


def ring_reduce_scatter(full, axis):
    n = lax.axis_size(axis)
    rows = full.shape[0] // n
    if n > 16:
        return lax.psum_scatter(
            full.astype(jnp.bfloat16), axis, scatter_dimension=0, tiled=True
        ).astype(jnp.float32)
    order, where, to_next, to_prev = ring_tables(n)
    me = lax.axis_index(axis)

    def chunk(shift):
        index = jnp.asarray([order[(where[d] + shift) % n] for d in range(n)], jnp.int32)[me]
        return lax.dynamic_slice_in_dim(full, index * rows, rows, axis=0)

    ahead = n // 2
    behind = n - 1 - ahead
    part_next = None
    part_prev = None
    for step in range(ahead):
        mine = chunk(ahead - step)
        part_next = mine if part_next is None else part_next.astype(jnp.float32) + mine
        part_next = lax.ppermute(part_next.astype(jnp.bfloat16), axis, to_next)
        if step < behind:
            mine = chunk(step - behind)
            part_prev = mine if part_prev is None else part_prev.astype(jnp.float32) + mine
            part_prev = lax.ppermute(part_prev.astype(jnp.bfloat16), axis, to_prev)
    total = lax.dynamic_slice_in_dim(full, me * rows, rows, axis=0) + part_next.astype(jnp.float32)
    if part_prev is not None:
        total = total + part_prev.astype(jnp.float32)
    return total


def tensor_sum(term, axis):
    n = lax.axis_size(axis)
    if n != 4:
        return lax.psum(term, axis).astype(jnp.float32)
    half = term.shape[0] // 2
    me = lax.axis_index(axis)
    core = me % 2
    keep = lax.dynamic_slice_in_dim(term, core * half, half, axis=0)
    give = lax.dynamic_slice_in_dim(term, (1 - core) * half, half, axis=0)
    on_chip = [(i, i ^ 1) for i in range(n)]
    across = [(i, i ^ 2) for i in range(n)]
    mine = keep.astype(jnp.float32) + lax.ppermute(give, axis, on_chip).astype(jnp.float32)
    total = mine + lax.ppermute(mine.astype(term.dtype), axis, across).astype(jnp.float32)
    back = lax.ppermute(total.astype(term.dtype), axis, on_chip).astype(jnp.float32)
    first = jnp.where(core == 0, total, back)
    second = jnp.where(core == 0, back, total)
    return jnp.concatenate([first, second], axis=0)


def on_device(
    tokens,
    piece_starts,
    attn_gain,
    w_query,
    w_key,
    w_value,
    w_outgate,
    w_forget,
    forget_bias,
    w_output,
    ffn_gain,
    w_gate,
    w_up,
    w_down,
    cotangent,
):
    sequences, length, width = tokens.shape
    heads_here = w_forget.shape[1]
    share_width = w_query.shape[1]
    head_size = share_width // heads_here
    row_count = sequences * length
    block = w_query.shape[0]
    units = w_gate.shape[1]

    def head_view(values):
        return values.reshape(sequences, length, heads_here, head_size)

    attn_local = jnp.concatenate(
        [w_output.T, w_query, w_key, w_value, w_outgate, w_forget, attn_gain[:, None]], axis=1
    )
    attn_full = ring_gather(attn_local, "dp")
    ffn_local = jnp.concatenate([w_gate, w_up, w_down.T, ffn_gain[:, None]], axis=1)
    ffn_local, attn_full = lax.optimization_barrier((ffn_local, attn_full))
    output_t = attn_full[:, :share_width]
    joined = attn_full[:, share_width : 5 * share_width]
    joined_five = attn_full[:, share_width : 5 * share_width + heads_here]
    forget_w = attn_full[:, 5 * share_width : 5 * share_width + heads_here]
    gain_one = attn_full[:, 5 * share_width + heads_here].astype(jnp.float32)
    ffn_full = lax.all_gather(ffn_local, "dp", axis=0, tiled=True)
    gate_up_w = ffn_full[:, : 2 * units]
    down_t = ffn_full[:, 2 * units : 3 * units]
    gain_two = ffn_full[:, 3 * units].astype(jnp.float32)

    inputs = tokens.reshape(row_count, width).astype(jnp.float32)
    scale_one = lax.rsqrt(jnp.mean(inputs * inputs, axis=-1, keepdims=True) + epsilon)
    unit_one = inputs * scale_one
    normed = (unit_one * gain_one).astype(jnp.bfloat16)
    projected = project(normed, joined)
    query_all = head_view(projected[:, :share_width].astype(jnp.bfloat16))
    key_all = head_view(projected[:, share_width : 2 * share_width].astype(jnp.bfloat16))
    value_all = head_view(projected[:, 2 * share_width : 3 * share_width].astype(jnp.bfloat16))
    gate_pre = projected[:, 3 * share_width :]
    forget_pre = project(normed, forget_w) + forget_bias[None, :]
    log_forget = jax.nn.log_sigmoid(forget_pre).reshape(sequences, length, heads_here)
    attended, normalizer = lax.map(
        attend_forward, (query_all, key_all, value_all, log_forget, piece_starts)
    )
    attended_flat = attended.reshape(row_count, share_width)
    gate_open = jax.nn.sigmoid(gate_pre)
    gated = (attended_flat * gate_open).astype(jnp.bfloat16)
    attention = tensor_sum(contract_cols(gated, output_t).astype(jnp.bfloat16), "tensor")
    hidden = inputs + attention
    scale_two = lax.rsqrt(jnp.mean(hidden * hidden, axis=-1, keepdims=True) + epsilon)
    unit_two = hidden * scale_two
    normed_two = (unit_two * gain_two).astype(jnp.bfloat16)
    inner_pre = project(normed_two, gate_up_w)
    gate_part = inner_pre[:, :units]
    up_part = inner_pre[:, units:]
    inner = (jax.nn.silu(gate_part) * up_part).astype(jnp.bfloat16)
    ffn_term = contract_cols(inner, down_t).astype(jnp.bfloat16)
    upstream_low = cotangent.reshape(row_count, width)
    upstream = upstream_low.astype(jnp.float32)
    grad_inner = project(upstream_low, down_t)
    sigma = jax.nn.sigmoid(gate_part)
    grad_gate = (grad_inner * up_part * sigma * (1.0 + gate_part * (1.0 - sigma))).astype(
        jnp.bfloat16
    )
    grad_up = (grad_inner * gate_part * sigma).astype(jnp.bfloat16)
    grad_gate_up = jnp.concatenate([grad_gate, grad_up], axis=1)
    grad_down_t = contract_rows(upstream_low, inner)
    grad_gate_up_w = contract_rows(normed_two, grad_gate_up)
    ffn_grads = jnp.concatenate([grad_gate_up_w, grad_down_t], axis=1).astype(jnp.bfloat16)
    grad_normed_two = tensor_sum(
        contract_cols(grad_gate_up, gate_up_w).astype(jnp.bfloat16), "tensor"
    )
    ffn_grads, grad_normed_two = lax.optimization_barrier((ffn_grads, grad_normed_two))
    ffn_sums = lax.psum_scatter(ffn_grads, "dp", scatter_dimension=0, tiled=True).astype(
        jnp.float32
    )
    ffn_term, grad_normed_two = lax.optimization_barrier((ffn_term, grad_normed_two))
    ffn_out = tensor_sum(ffn_term, "tensor")
    grad_unit_two = grad_normed_two * gain_two
    grad_hidden = upstream + scale_two * (
        grad_unit_two - unit_two * jnp.mean(grad_unit_two * unit_two, axis=-1, keepdims=True)
    )
    hidden_low = grad_hidden.astype(jnp.bfloat16)
    grad_output_t = contract_rows(hidden_low, gated)
    grad_gated = project(hidden_low, output_t)
    grad_attended = (grad_gated * gate_open).astype(jnp.bfloat16)
    grad_gate_pre = (grad_gated * attended_flat * gate_open * (1.0 - gate_open)).astype(
        jnp.bfloat16
    )
    grad_query, grad_key, grad_value, grad_log = lax.map(
        attend_backward,
        (
            query_all,
            key_all,
            value_all,
            log_forget,
            piece_starts,
            attended,
            normalizer,
            head_view(grad_attended),
        ),
    )
    grad_forget = (grad_log.reshape(row_count, heads_here) * jax.nn.sigmoid(-forget_pre)).astype(
        jnp.bfloat16
    )
    grad_five = jnp.concatenate(
        [
            grad_query.reshape(row_count, share_width),
            grad_key.reshape(row_count, share_width),
            grad_value.reshape(row_count, share_width),
            grad_gate_pre,
            grad_forget,
        ],
        axis=1,
    )
    output = (hidden + ffn_out).astype(jnp.bfloat16).reshape(tokens.shape)
    grad_bias = jnp.sum(grad_forget.astype(jnp.float32), axis=0)
    place = jnp.arange(width, dtype=jnp.int32) % block
    bias_col = jnp.where(
        place < heads_here, jnp.take(grad_bias, jnp.minimum(place, heads_here - 1)), 0.0
    )
    late_normed_two, grad_five = lax.optimization_barrier((grad_normed_two, grad_five))
    grad_ffn_gain = jnp.sum(late_normed_two * unit_two, axis=0)
    late_grads = lax.dot_general(
        grad_five, normed, (((0,), (0,)), ((), ())), preferred_element_type=jnp.float32
    ).T
    grad_normed = tensor_sum(contract_cols(grad_five, joined_five).astype(jnp.bfloat16), "tensor")
    grad_attn_gain = jnp.sum(grad_normed * unit_one, axis=0)
    late_sums = ring_reduce_scatter(
        jnp.concatenate(
            [
                late_grads.astype(jnp.bfloat16),
                bias_col[:, None].astype(jnp.bfloat16),
                grad_attn_gain[:, None].astype(jnp.bfloat16),
                grad_ffn_gain[:, None].astype(jnp.bfloat16),
                grad_output_t.astype(jnp.bfloat16),
            ],
            axis=1,
        ),
        "dp",
    )
    out_at = 4 * share_width + heads_here + 3
    grad_unit_one = grad_normed * gain_one
    grad_inputs = grad_hidden + scale_one * (
        grad_unit_one - unit_one * jnp.mean(grad_unit_one * unit_one, axis=-1, keepdims=True)
    )
    tokens_grad = grad_inputs.astype(jnp.bfloat16).reshape(tokens.shape)
    forget_at = 4 * share_width
    return (
        output,
        tokens_grad,
        late_sums[:, forget_at + heads_here + 1],
        late_sums[:, :share_width],
        late_sums[:, share_width : 2 * share_width],
        late_sums[:, 2 * share_width : 3 * share_width],
        late_sums[:, 3 * share_width : 4 * share_width],
        late_sums[:, forget_at : forget_at + heads_here],
        late_sums[:heads_here, forget_at + heads_here],
        late_sums[:, out_at : out_at + share_width].T,
        late_sums[:, out_at - 1],
        ffn_sums[:, :units],
        ffn_sums[:, units : 2 * units],
        ffn_sums[:, 2 * units : 3 * units].T,
    )


def solution(mesh):
    placed = (
        P("dp", None, None),
        P("dp", None),
        P("dp"),
        P("dp", "tensor"),
        P("dp", "tensor"),
        P("dp", "tensor"),
        P("dp", "tensor"),
        P("dp", "tensor"),
        P("tensor"),
        P("tensor", "dp"),
        P("dp"),
        P("dp", "tensor"),
        P("dp", "tensor"),
        P("tensor", "dp"),
        P("dp", None, None),
    )
    return jax.shard_map(
        on_device,
        mesh=mesh,
        in_specs=placed,
        out_specs=(
            P("dp", None, None),
            P("dp", None, None),
            P("dp"),
            P("dp", "tensor"),
            P("dp", "tensor"),
            P("dp", "tensor"),
            P("dp", "tensor"),
            P("dp", "tensor"),
            P("tensor"),
            P("tensor", "dp"),
            P("dp"),
            P("dp", "tensor"),
            P("dp", "tensor"),
            P("tensor", "dp"),
        ),
        check_vma=False,
    )
```
